32 devices in a mesh: seq: 8 (over z, x), head: 4 (over y, core).
Axes of the slice: x: 2, y: 2, z: 4, core: 2. Of those that a mesh axis runs over, the one named last changes fastest.
Arguments:
- queries: float32 [8192, 2048], P('seq', 'head')
- keys: float32 [8192, 2048], P('seq', 'head')
- values: float32 [8192, 2048], P('seq', 'head'), may hold values from -6 to 6
- positions: int32 [8192], P('seq'), may hold values from 0 to 8191, as said below
- cluster: int32 [8192], P('seq'), may hold values from 0 to 7, as said below
- slot: int32 [8192], P('seq'), may hold values from 0 to 1023, as said below
- out_weight: float32 [2048, 4096], P('head'), may hold values from -0.5 to 0.5
Outputs:
- projected: float32 [8192, 4096], P('seq', 'head')
The draws below stay inside these ranges and needn't reach their ends.
Inputs may be any that keep to these rules, and one draw needn't show every extreme that they name: Every cluster holds exactly 1024 tokens. Of the tokens of one index of seq, at most 192 have cluster ids in one range k * 1 to (k + 1) - 1. Within each cluster every slot is taken once, in increasing order of position. `positions`: each position is taken by exactly one token.
All inputs are finite; a program needn't handle non-finite values.
Results may differ from the reference program's by a relative error of at most 0.0003.
Values sent between devices are 32-bit elements; how exact they have to be, the bound alone decides.
No kernel may reach another device: no remote copies, remote signals or barrier semaphores. Data moves between devices by JAX's collectives and lax.ppermute only.
A program may use at most 128 MiB of HBM per device.

```python
import math
import jax
import jax.numpy as jnp
from jax import lax

D = 4096
H = 16
DH = 128
CS = 1024
CL_DEV = 1
NC = 8
TOK_DEV = 1024
TOKENS = 8192


def routing_tables(key):
    owners = NC // CL_DEV
    base_count = TOK_DEV // owners
    half_count = base_count // 2
    first, second, third, fourth = jax.random.split(jax.random.fold_in(key, 7), 4)
    sigma = jax.random.permutation(first, owners)
    owner_idx = jnp.arange(owners)
    counts = jnp.full((owners, owners), base_count, jnp.int32)
    counts = counts.at[owner_idx, sigma].add(half_count)
    counts = counts.at[owner_idx, sigma[(owner_idx + 1) % owners]].add(-half_count)
    ends = jnp.cumsum(counts, axis=1)
    within = jnp.arange(TOK_DEV)
    owner_rows = jnp.sum((within[None, None, :] >= ends[:, :, None]).astype(jnp.int32), axis=1)
    shuffled = jax.vmap(jax.random.permutation)(jax.random.split(second, owners), owner_rows)
    owner_flat = shuffled.reshape(-1).astype(jnp.int32)
    sorted_idx = jnp.argsort(owner_flat, stable=True)

    def one_perm(subkey):
        return jax.random.permutation(subkey, TOK_DEV)
    perms = jax.vmap(one_perm)(jax.random.split(third, owners)).reshape(-1).astype(jnp.int32)
    local_idx = jnp.zeros((TOKENS,), jnp.int32).at[sorted_idx].set(perms)
    cluster_ids = owner_flat * CL_DEV + local_idx // CS
    token_pos = jax.random.permutation(fourth, TOKENS).astype(jnp.int32)
    order = jnp.argsort(cluster_ids * TOKENS + token_pos)
    slots = jnp.zeros((TOKENS,), jnp.int32).at[order].set((jnp.arange(TOKENS) % CS).astype(jnp.int32))
    return (cluster_ids, slots, token_pos)


def paired_draw(key):
    query_key, key_key = jax.random.split(jax.random.fold_in(key, 11), 2)
    shape = (TOKENS, H * DH)
    query_arr = jnp.clip(jax.random.normal(query_key, shape, jnp.float32), -6.0, 6.0)
    key_arr = jnp.clip(jax.random.normal(key_key, shape, jnp.float32), -6.0, 6.0)
    return (query_arr, key_arr)


def draw_queries(key, part):
    return paired_draw(key)[0]


def draw_keys(key, part):
    return paired_draw(key)[1]


def draw_positions(key, part):
    return routing_tables(key)[2]


def draw_cluster(key, part):
    return routing_tables(key)[0]


def draw_slot(key, part):
    return routing_tables(key)[1]


def levels(key, dims, cuts, least, largest):
    level = 1.0
    for dim, blocks in cuts:
        draws = jax.random.uniform(jax.random.fold_in(jax.random.fold_in(key, 6), dim), (blocks,), jnp.float32, least / len(cuts), largest / len(cuts))
        level = level * jnp.repeat(jnp.exp(draws), dims[dim] // blocks).reshape((-1,) + (1,) * (len(dims) - 1 - dim))
    return level


def scatter_about(key, shape, spread, reach, cuts=(), kind=jnp.bfloat16):
    factor_of = levels(key, shape, cuts, -0.22, 0.18) if cuts else 1.0
    array = jax.random.normal(key, shape, jnp.float32) * spread * factor_of
    return jnp.minimum(jnp.maximum(array, -reach), reach).astype(kind)


def setup_inputs(seed: int = 0) -> dict:
    key_list = jax.random.split(jax.random.key(seed), 8)
    queries = draw_queries(jax.random.fold_in(key_list[7], 71), 0)
    keys = draw_keys(jax.random.fold_in(key_list[7], 71), 0)
    values = scatter_about(key_list[2], (TOKENS, H * DH), 1.0, 6.0, ((0, 8), (1, 4)), jnp.float32)
    positions = draw_positions(jax.random.fold_in(key_list[7], 71), 0)
    cluster = draw_cluster(jax.random.fold_in(key_list[7], 71), 0)
    slot = draw_slot(jax.random.fold_in(key_list[7], 71), 0)
    out_weight = scatter_about(key_list[6], (H * DH, D), (H * DH // 16) ** -0.5, 0.5, ((0, 4),), jnp.float32)
    return {"queries": queries, "keys": keys, "values": values, "positions": positions, "cluster": cluster, "slot": slot, "out_weight": out_weight}


ROPE_BASE = 500000.0
ORIG_CONTEXT = 8192.0
STRETCH = 4.0
BETA_FAST = 32.0
BETA_SLOW = 1.0

def yarn_tables(token_pos, width):
    half_width = width // 2
    expo = jnp.arange(half_width, dtype=jnp.float32) * 2.0 / width
    theta = jnp.exp(-expo * math.log(ROPE_BASE))
    ratio = ORIG_CONTEXT * theta / (2.0 * math.pi)
    ramp = jnp.clip((ratio - BETA_SLOW) / (BETA_FAST - BETA_SLOW), 0.0, 1.0)
    freq = theta * (ramp + (1.0 - ramp) / STRETCH)
    angle = token_pos.astype(jnp.float32)[:, None] * freq[None, :]
    mscale = 0.1 * math.log(STRETCH) + 1.0
    cos_table = jnp.concatenate([jnp.cos(angle), jnp.cos(angle)], -1) * mscale
    sin_table = jnp.concatenate([jnp.sin(angle), jnp.sin(angle)], -1) * mscale
    return (cos_table[:, None, :], sin_table[:, None, :])

def rotate(field, cos_table, sin_table):
    half_width = field.shape[-1] // 2
    turned = jnp.concatenate([-field[..., half_width:], field[..., :half_width]], -1)
    return field * cos_table + turned * sin_table

def cluster_attention(triple):
    query_c, key_c, value_c = triple
    length = query_c.shape[0]
    scores = jnp.einsum('qhd,khd->hqk', query_c, key_c, precision=lax.Precision.HIGHEST) / math.sqrt(query_c.shape[-1])
    causal = jnp.arange(length)[:, None] >= jnp.arange(length)[None, :]
    scores = jnp.where(causal[None], scores, -jnp.inf)
    peak = lax.optimization_barrier(jnp.max(scores, -1, keepdims=True))
    weights = jnp.exp(scores - peak)
    total = lax.optimization_barrier(jnp.sum(weights, -1, keepdims=True))
    summed = jnp.einsum('hqk,khd->qhd', weights, value_c, precision=lax.Precision.HIGHEST)
    return summed / jnp.transpose(total, (1, 0, 2))

def reference(queries, keys, values, positions, cluster, slot, out_weight):
    cos_table, sin_table = yarn_tables(positions, DH)
    shaped = (TOKENS, H, DH)
    rot_q = rotate(queries.reshape(shaped), cos_table, sin_table)
    rot_k = rotate(keys.reshape(shaped), cos_table, sin_table)
    sorted_rows = jnp.argsort(cluster * CS + slot).astype(jnp.int32)
    grouped = (rot_q[sorted_rows].reshape(NC, CS, H, DH), rot_k[sorted_rows].reshape(NC, CS, H, DH), values.reshape(shaped)[sorted_rows].reshape(NC, CS, H, DH))
    attended = lax.map(cluster_attention, grouped)
    mixed = jnp.zeros((TOKENS, H * DH), jnp.float32).at[sorted_rows].set(attended.reshape(TOKENS, H * DH))
    return jnp.dot(mixed, out_weight, precision=lax.Precision.HIGHEST, preferred_element_type=jnp.float32)
```

```python
import math

import jax
import jax.numpy as jnp
from jax import lax
from jax.sharding import PartitionSpec as P

DH = 128
CS = 1024
CL_DEV = 1


ROPE_BASE = 500000.0
ORIG_CONTEXT = 8192.0
STRETCH = 4.0
BETA_FAST = 32.0
BETA_SLOW = 1.0


def yarn_tables(token_pos, width):
    half_width = width // 2
    expo = jnp.arange(half_width, dtype=jnp.float32) * 2.0 / width
    theta = jnp.exp(-expo * math.log(ROPE_BASE))
    ratio = ORIG_CONTEXT * theta / (2.0 * math.pi)
    ramp = jnp.clip((ratio - BETA_SLOW) / (BETA_FAST - BETA_SLOW), 0.0, 1.0)
    freq = theta * (ramp + (1.0 - ramp) / STRETCH)
    angle = token_pos.astype(jnp.float32)[:, None] * freq[None, :]
    mscale = 0.1 * math.log(STRETCH) + 1.0
    cos_table = jnp.concatenate([jnp.cos(angle), jnp.cos(angle)], -1) * mscale
    sin_table = jnp.concatenate([jnp.sin(angle), jnp.sin(angle)], -1) * mscale
    return (cos_table[:, None, :], sin_table[:, None, :])


def rotate(field, cos_table, sin_table):
    half_width = field.shape[-1] // 2
    turned = jnp.concatenate([-field[..., half_width:], field[..., :half_width]], -1)
    return field * cos_table + turned * sin_table


def cluster_attention(triple):
    query_c, key_c, value_c = triple
    length = query_c.shape[0]
    scores = jnp.einsum(
        "qhd,khd->hqk", query_c, key_c, precision=lax.Precision.HIGHEST
    ) / math.sqrt(query_c.shape[-1])
    causal = jnp.arange(length)[:, None] >= jnp.arange(length)[None, :]
    scores = jnp.where(causal[None], scores, -jnp.inf)
    peak = jnp.max(scores, -1, keepdims=True)
    weights = jnp.exp(scores - peak)
    total = jnp.sum(weights, -1, keepdims=True)
    summed = jnp.einsum("hqk,khd->qhd", weights, value_c, precision=lax.Precision.HIGHEST)
    return summed / jnp.transpose(total, (1, 0, 2))


def attend_local(query_all, key_all, value_all):
    row_count, head_count, width = query_all.shape
    grouped = (
        query_all.reshape(row_count // CS, CS, head_count, width),
        key_all.reshape(row_count // CS, CS, head_count, width),
        value_all.reshape(row_count // CS, CS, head_count, width),
    )
    return lax.map(cluster_attention, grouped).reshape(row_count, head_count, width)


def per_device(queries, keys, values, positions, cluster, slot, out_weight):
    seq_count = lax.axis_size("seq")
    head_count = lax.axis_size("head")
    head_index = lax.axis_index("head")
    col_width = out_weight.shape[1] // head_count
    weight_blocks = out_weight.reshape(out_weight.shape[0], head_count, col_width)
    weight_parts = [None] * head_count
    for shift in range(head_count):
        if shift == 0:
            piece = weight_blocks[:, head_index]
        else:
            dest = (head_index + shift) % head_count
            piece = lax.ppermute(
                jnp.take(weight_blocks, dest, axis=1),
                "head",
                [(src, (src + shift) % head_count) for src in range(head_count)],
            )
        weight_parts[shift] = piece
    stacked_w = jnp.stack(weight_parts, 0)
    order = (head_index - jnp.arange(head_count)) % head_count
    weight_cols = stacked_w[order].reshape(head_count * out_weight.shape[0], col_width)
    row_count = queries.shape[0]
    capacity = 3 * row_count // (2 * seq_count)
    buffer_rows = seq_count * capacity
    heads_here = queries.shape[1] // DH
    owner_ids = cluster // CL_DEV
    target_row = cluster % CL_DEV * CS + slot
    one_hot = (owner_ids[:, None] == jnp.arange(seq_count)[None, :]).astype(jnp.int32)
    token_rank = jnp.sum(jnp.cumsum(one_hot, 0) * one_hot, 1) - 1
    send_row = owner_ids * capacity + token_rank
    source_token = (
        jnp.full((buffer_rows,), row_count, jnp.int32)
        .at[send_row]
        .set(jnp.arange(row_count, dtype=jnp.int32))
    )
    cos_table, sin_table = yarn_tables(positions, DH)
    shaped = (row_count, heads_here, DH)
    rot_q = rotate(queries.reshape(shaped), cos_table, sin_table)
    rot_k = rotate(keys.reshape(shaped), cos_table, sin_table)
    stacked = jnp.concatenate([rot_q, rot_k, values.reshape(shaped)], 1)
    stacked = jnp.concatenate([stacked, jnp.zeros((1, 3 * heads_here, DH), jnp.float32)], 0)
    send_all = stacked[source_token]
    send_q = send_all[:, :heads_here]
    send_k = send_all[:, heads_here : 2 * heads_here]
    send_v = send_all[:, 2 * heads_here :]
    slot_rows = jnp.full((buffer_rows,), row_count, jnp.int32).at[send_row].set(target_row)
    arrived = lax.all_to_all(slot_rows, "seq", split_axis=0, concat_axis=0, tiled=True)
    picked = jnp.minimum(arrived, row_count - 1)
    where_from = (
        jnp.zeros((row_count,), jnp.int32)
        .at[arrived]
        .set(jnp.arange(buffer_rows, dtype=jnp.int32), mode="drop")
    )

    def place(pieces):
        return pieces[where_from]

    received = (
        lax.all_to_all(send_q, "seq", split_axis=0, concat_axis=0, tiled=True),
        lax.all_to_all(send_k, "seq", split_axis=0, concat_axis=0, tiled=True),
        lax.all_to_all(send_v, "seq", split_axis=0, concat_axis=0, tiled=True),
    )
    result = attend_local(place(received[0]), place(received[1]), place(received[2]))
    result, weight_cols = lax.optimization_barrier((result, weight_cols))
    returned = lax.all_to_all(result[picked], "seq", split_axis=0, concat_axis=0, tiled=True)
    mixed = returned[send_row].reshape(row_count, heads_here * DH)
    gathered = lax.all_gather(mixed, "head", axis=1, tiled=True)
    projected = jnp.dot(
        gathered, weight_cols, precision=lax.Precision.HIGHEST, preferred_element_type=jnp.float32
    )
    return projected


def solution(mesh):
    in_specs = (
        P("seq", "head"),
        P("seq", "head"),
        P("seq", "head"),
        P("seq"),
        P("seq"),
        P("seq"),
        P("head", None),
    )
    out_specs = P("seq", "head")
    return jax.shard_map(
        per_device, mesh=mesh, in_specs=in_specs, out_specs=out_specs, check_vma=False
    )
```

```python
import math

import jax
import jax.numpy as jnp
from jax import lax
from jax.sharding import PartitionSpec as P

DH = 128
CS = 1024
CL_DEV = 1


ROPE_BASE = 500000.0
ORIG_CONTEXT = 8192.0
STRETCH = 4.0
BETA_FAST = 32.0
BETA_SLOW = 1.0


def yarn_tables(token_pos, width):
    half_width = width // 2
    expo = jnp.arange(half_width, dtype=jnp.float32) * 2.0 / width
    theta = jnp.exp(-expo * math.log(ROPE_BASE))
    ratio = ORIG_CONTEXT * theta / (2.0 * math.pi)
    ramp = jnp.clip((ratio - BETA_SLOW) / (BETA_FAST - BETA_SLOW), 0.0, 1.0)
    freq = theta * (ramp + (1.0 - ramp) / STRETCH)
    angle = token_pos.astype(jnp.float32)[:, None] * freq[None, :]
    mscale = 0.1 * math.log(STRETCH) + 1.0
    cos_table = jnp.concatenate([jnp.cos(angle), jnp.cos(angle)], -1) * mscale
    sin_table = jnp.concatenate([jnp.sin(angle), jnp.sin(angle)], -1) * mscale
    return (cos_table[:, None, :], sin_table[:, None, :])


def rotate(field, cos_table, sin_table):
    half_width = field.shape[-1] // 2
    turned = jnp.concatenate([-field[..., half_width:], field[..., :half_width]], -1)
    return field * cos_table + turned * sin_table


def cluster_attention(triple):
    query_c, key_c, value_c = triple
    length = query_c.shape[0]
    scores = jnp.einsum(
        "qhd,khd->hqk", query_c, key_c, precision=lax.Precision.HIGHEST
    ) / math.sqrt(query_c.shape[-1])
    causal = jnp.arange(length)[:, None] >= jnp.arange(length)[None, :]
    scores = jnp.where(causal[None], scores, -jnp.inf)
    peak = jnp.max(scores, -1, keepdims=True)
    weights = jnp.exp(scores - peak)
    total = jnp.sum(weights, -1, keepdims=True)
    summed = jnp.einsum("hqk,khd->qhd", weights, value_c, precision=lax.Precision.HIGHEST)
    return summed / jnp.transpose(total, (1, 0, 2))


def attend_local(query_all, key_all, value_all):
    row_count, head_count, width = query_all.shape
    grouped = (
        query_all.reshape(row_count // CS, CS, head_count, width),
        key_all.reshape(row_count // CS, CS, head_count, width),
        value_all.reshape(row_count // CS, CS, head_count, width),
    )
    return lax.map(cluster_attention, grouped).reshape(row_count, head_count, width)


def per_device(queries, keys, values, positions, cluster, slot, out_weight):
    seq_count = lax.axis_size("seq")
    weight_cols = lax.all_to_all(out_weight, "head", split_axis=1, concat_axis=0, tiled=True)
    row_count = queries.shape[0]
    capacity = 3 * row_count // (2 * seq_count)
    buffer_rows = seq_count * capacity
    heads_here = queries.shape[1] // DH
    owner_ids = cluster // CL_DEV
    target_row = cluster % CL_DEV * CS + slot
    one_hot = (owner_ids[:, None] == jnp.arange(seq_count)[None, :]).astype(jnp.int32)
    token_rank = jnp.sum(jnp.cumsum(one_hot, 0) * one_hot, 1) - 1
    send_row = owner_ids * capacity + token_rank
    source_token = (
        jnp.full((buffer_rows,), row_count, jnp.int32)
        .at[send_row]
        .set(jnp.arange(row_count, dtype=jnp.int32))
    )
    cos_table, sin_table = yarn_tables(positions, DH)
    shaped = (row_count, heads_here, DH)
    rot_q = rotate(queries.reshape(shaped), cos_table, sin_table)
    rot_k = rotate(keys.reshape(shaped), cos_table, sin_table)
    stacked = jnp.concatenate([rot_q, rot_k, values.reshape(shaped)], 1)
    stacked = jnp.concatenate([stacked, jnp.zeros((1, 3 * heads_here, DH), jnp.float32)], 0)
    send_all = stacked[source_token]
    send_q = send_all[:, :heads_here]
    send_k = send_all[:, heads_here : 2 * heads_here]
    send_v = send_all[:, 2 * heads_here :]
    slot_rows = jnp.full((buffer_rows,), row_count, jnp.int32).at[send_row].set(target_row)
    arrived = lax.all_to_all(slot_rows, "seq", split_axis=0, concat_axis=0, tiled=True)
    picked = jnp.minimum(arrived, row_count - 1)
    where_from = (
        jnp.zeros((row_count,), jnp.int32)
        .at[arrived]
        .set(jnp.arange(buffer_rows, dtype=jnp.int32), mode="drop")
    )

    def place(pieces):
        return pieces[where_from]

    received = (
        lax.all_to_all(send_q, "seq", split_axis=0, concat_axis=0, tiled=True),
        lax.all_to_all(send_k, "seq", split_axis=0, concat_axis=0, tiled=True),
        lax.all_to_all(send_v, "seq", split_axis=0, concat_axis=0, tiled=True),
    )
    result = attend_local(place(received[0]), place(received[1]), place(received[2]))
    result, weight_cols = lax.optimization_barrier((result, weight_cols))
    returned = lax.all_to_all(result[picked], "seq", split_axis=0, concat_axis=0, tiled=True)
    mixed = returned[send_row].reshape(row_count, heads_here * DH)
    gathered = lax.all_gather(mixed, "head", axis=1, tiled=True)
    projected = jnp.dot(
        gathered, weight_cols, precision=lax.Precision.HIGHEST, preferred_element_type=jnp.float32
    )
    return projected


def solution(mesh):
    in_specs = (
        P("seq", "head"),
        P("seq", "head"),
        P("seq", "head"),
        P("seq"),
        P("seq"),
        P("seq"),
        P("head", None),
    )
    out_specs = P("seq", "head")
    return jax.shard_map(
        per_device, mesh=mesh, in_specs=in_specs, out_specs=out_specs, check_vma=False
    )
```

```python
import math

import jax
import jax.numpy as jnp
from jax import lax
from jax.sharding import PartitionSpec as P

DH = 128
CS = 1024
CL_DEV = 1


ROPE_BASE = 500000.0
ORIG_CONTEXT = 8192.0
STRETCH = 4.0
BETA_FAST = 32.0
BETA_SLOW = 1.0


def yarn_tables(token_pos, width):
    half_width = width // 2
    expo = jnp.arange(half_width, dtype=jnp.float32) * 2.0 / width
    theta = jnp.exp(-expo * math.log(ROPE_BASE))
    ratio = ORIG_CONTEXT * theta / (2.0 * math.pi)
    ramp = jnp.clip((ratio - BETA_SLOW) / (BETA_FAST - BETA_SLOW), 0.0, 1.0)
    freq = theta * (ramp + (1.0 - ramp) / STRETCH)
    angle = token_pos.astype(jnp.float32)[:, None] * freq[None, :]
    mscale = 0.1 * math.log(STRETCH) + 1.0
    cos_table = jnp.concatenate([jnp.cos(angle), jnp.cos(angle)], -1) * mscale
    sin_table = jnp.concatenate([jnp.sin(angle), jnp.sin(angle)], -1) * mscale
    return (cos_table[:, None, :], sin_table[:, None, :])


def rotate(field, cos_table, sin_table):
    half_width = field.shape[-1] // 2
    turned = jnp.concatenate([-field[..., half_width:], field[..., :half_width]], -1)
    return field * cos_table + turned * sin_table


def cluster_attention(triple):
    query_c, key_c, value_c = triple
    length = query_c.shape[0]
    scores = jnp.einsum(
        "qhd,khd->hqk", query_c, key_c, precision=lax.Precision.HIGH
    ) / math.sqrt(query_c.shape[-1])
    causal = jnp.arange(length)[:, None] >= jnp.arange(length)[None, :]
    scores = jnp.where(causal[None], scores, -jnp.inf)
    peak = jnp.max(scores, -1, keepdims=True)
    weights = jnp.exp(scores - peak)
    total = jnp.sum(weights, -1, keepdims=True)
    summed = jnp.einsum("hqk,khd->qhd", weights, value_c, precision=lax.Precision.HIGH)
    return summed / jnp.transpose(total, (1, 0, 2))


def attend_local(query_all, key_all, value_all):
    row_count, head_count, width = query_all.shape
    grouped = (
        query_all.reshape(row_count // CS, CS, head_count, width),
        key_all.reshape(row_count // CS, CS, head_count, width),
        value_all.reshape(row_count // CS, CS, head_count, width),
    )
    return lax.map(cluster_attention, grouped).reshape(row_count, head_count, width)


def per_device(queries, keys, values, positions, cluster, slot, out_weight):
    seq_count = lax.axis_size("seq")
    row_count = queries.shape[0]
    capacity = 3 * row_count // (2 * seq_count)
    buffer_rows = seq_count * capacity
    heads_here = queries.shape[1] // DH
    owner_ids = cluster // CL_DEV
    target_row = cluster % CL_DEV * CS + slot
    one_hot = (owner_ids[:, None] == jnp.arange(seq_count)[None, :]).astype(jnp.int32)
    token_rank = jnp.sum(jnp.cumsum(one_hot, 0) * one_hot, 1) - 1
    send_row = owner_ids * capacity + token_rank
    source_token = (
        jnp.full((buffer_rows,), row_count, jnp.int32)
        .at[send_row]
        .set(jnp.arange(row_count, dtype=jnp.int32))
    )
    cos_table, sin_table = yarn_tables(positions, DH)
    shaped = (row_count, heads_here, DH)
    rot_q = rotate(queries.reshape(shaped), cos_table, sin_table)
    rot_k = rotate(keys.reshape(shaped), cos_table, sin_table)
    stacked = jnp.concatenate([rot_q, rot_k, values.reshape(shaped)], 1)
    stacked = jnp.concatenate([stacked, jnp.zeros((1, 3 * heads_here, DH), jnp.float32)], 0)
    send_all = stacked[source_token]
    send_q = send_all[:, :heads_here]
    send_k = send_all[:, heads_here : 2 * heads_here]
    send_v = send_all[:, 2 * heads_here :]
    slot_rows = jnp.full((buffer_rows,), row_count, jnp.int32).at[send_row].set(target_row)
    arrived = lax.all_to_all(slot_rows, "seq", split_axis=0, concat_axis=0, tiled=True)
    picked = jnp.minimum(arrived, row_count - 1)
    where_from = (
        jnp.zeros((row_count,), jnp.int32)
        .at[arrived]
        .set(jnp.arange(buffer_rows, dtype=jnp.int32), mode="drop")
    )

    def place(pieces):
        return pieces[where_from]

    received = (
        lax.all_to_all(send_q, "seq", split_axis=0, concat_axis=0, tiled=True),
        lax.all_to_all(send_k, "seq", split_axis=0, concat_axis=0, tiled=True),
        lax.all_to_all(send_v, "seq", split_axis=0, concat_axis=0, tiled=True),
    )
    result = attend_local(place(received[0]), place(received[1]), place(received[2]))
    returned = lax.all_to_all(result[picked], "seq", split_axis=0, concat_axis=0, tiled=True)
    mixed = returned[send_row].reshape(row_count, heads_here * DH)
    return project_scatter(mixed, out_weight)


def swap_pairs(count, bit):
    return [(index, index ^ bit) for index in range(count)]


def project_scatter(mixed, out_weight):
    head_count = lax.axis_size("head")
    head_index = lax.axis_index("head")
    core = head_index % 2
    y_half = head_index // 2
    in_rows, total_cols = out_weight.shape
    width = total_cols // head_count
    blocks = out_weight.reshape(in_rows, head_count // 2, 2, width)
    other_w = jnp.where(core == 0, blocks[:, :, 1], blocks[:, :, 0])
    own_w = jnp.where(core == 0, blocks[:, :, 0], blocks[:, :, 1])
    other_w = other_w.reshape(in_rows, total_cols // 2)
    own_w = own_w.reshape(in_rows, total_cols // 2)
    dot = lambda a, b: jnp.dot(
        a, b, precision=lax.Precision.HIGH, preferred_element_type=jnp.float32
    )
    to_partner = dot(mixed, other_w)
    from_partner = lax.ppermute(to_partner, "head", swap_pairs(head_count, 1))
    chip_sum = dot(mixed, own_w) + from_partner
    halves = chip_sum.reshape(chip_sum.shape[0], head_count // 2, width)
    send_half = jnp.where(y_half == 0, halves[:, 1], halves[:, 0])
    keep_half = jnp.where(y_half == 0, halves[:, 0], halves[:, 1])
    from_across = lax.ppermute(send_half, "head", swap_pairs(head_count, 2))
    return keep_half + from_across


def solution(mesh):
    in_specs = (
        P("seq", "head"),
        P("seq", "head"),
        P("seq", "head"),
        P("seq"),
        P("seq"),
        P("seq"),
        P("head", None),
    )
    out_specs = P("seq", "head")
    return jax.shard_map(
        per_device, mesh=mesh, in_specs=in_specs, out_specs=out_specs, check_vma=False
    )
```

```python
import math

import jax
import jax.numpy as jnp
from jax import lax
from jax.sharding import PartitionSpec as P

DH = 128
CS = 1024
CL_DEV = 1


ROPE_BASE = 500000.0
ORIG_CONTEXT = 8192.0
STRETCH = 4.0
BETA_FAST = 32.0
BETA_SLOW = 1.0


def yarn_tables(token_pos, width):
    half_width = width // 2
    expo = jnp.arange(half_width, dtype=jnp.float32) * 2.0 / width
    theta = jnp.exp(-expo * math.log(ROPE_BASE))
    ratio = ORIG_CONTEXT * theta / (2.0 * math.pi)
    ramp = jnp.clip((ratio - BETA_SLOW) / (BETA_FAST - BETA_SLOW), 0.0, 1.0)
    freq = theta * (ramp + (1.0 - ramp) / STRETCH)
    angle = token_pos.astype(jnp.float32)[:, None] * freq[None, :]
    mscale = 0.1 * math.log(STRETCH) + 1.0
    cos_table = jnp.concatenate([jnp.cos(angle), jnp.cos(angle)], -1) * mscale
    sin_table = jnp.concatenate([jnp.sin(angle), jnp.sin(angle)], -1) * mscale
    return (cos_table[:, None, :], sin_table[:, None, :])


def rotate(field, cos_table, sin_table):
    half_width = field.shape[-1] // 2
    turned = jnp.concatenate([-field[..., half_width:], field[..., :half_width]], -1)
    return field * cos_table + turned * sin_table


def cluster_attention(triple):
    query_c, key_c, value_c = triple
    length = query_c.shape[0]
    scores = jnp.einsum(
        "qhd,khd->hqk", query_c, key_c, precision=lax.Precision.HIGH
    ) / math.sqrt(query_c.shape[-1])
    causal = jnp.arange(length)[:, None] >= jnp.arange(length)[None, :]
    scores = jnp.where(causal[None], scores, -jnp.inf)
    peak = jnp.max(scores, -1, keepdims=True)
    weights = jnp.exp(scores - peak)
    total = jnp.sum(weights, -1, keepdims=True)
    summed = jnp.einsum("hqk,khd->qhd", weights, value_c, precision=lax.Precision.HIGH)
    return summed / jnp.transpose(total, (1, 0, 2))


def attend_local(query_all, key_all, value_all):
    row_count, head_count, width = query_all.shape
    grouped = (
        query_all.reshape(row_count // CS, CS, head_count, width),
        key_all.reshape(row_count // CS, CS, head_count, width),
        value_all.reshape(row_count // CS, CS, head_count, width),
    )
    return lax.map(cluster_attention, grouped).reshape(row_count, head_count, width)


def per_device(queries, keys, values, positions, cluster, slot, out_weight):
    seq_count = lax.axis_size("seq")
    row_count = queries.shape[0]
    capacity = 3 * row_count // (2 * seq_count)
    buffer_rows = seq_count * capacity
    heads_here = queries.shape[1] // DH
    owner_ids = cluster // CL_DEV
    target_row = cluster % CL_DEV * CS + slot
    one_hot = (owner_ids[:, None] == jnp.arange(seq_count)[None, :]).astype(jnp.int32)
    token_rank = jnp.sum(jnp.cumsum(one_hot, 0) * one_hot, 1) - 1
    send_row = owner_ids * capacity + token_rank
    source_token = (
        jnp.full((buffer_rows,), row_count, jnp.int32)
        .at[send_row]
        .set(jnp.arange(row_count, dtype=jnp.int32))
    )
    cos_table, sin_table = yarn_tables(positions, DH)
    shaped = (row_count, heads_here, DH)
    rot_q = rotate(queries.reshape(shaped), cos_table, sin_table)
    rot_k = rotate(keys.reshape(shaped), cos_table, sin_table)
    stacked = jnp.concatenate([rot_q, rot_k, values.reshape(shaped)], 1)
    stacked = jnp.concatenate([stacked, jnp.zeros((1, 3 * heads_here, DH), jnp.float32)], 0)
    send_all = stacked[source_token]
    send_q = send_all[:, :heads_here]
    send_k = send_all[:, heads_here : 2 * heads_here]
    send_v = send_all[:, 2 * heads_here :]
    slot_rows = jnp.full((buffer_rows,), row_count, jnp.int32).at[send_row].set(target_row)
    arrived = lax.all_to_all(slot_rows, "seq", split_axis=0, concat_axis=0, tiled=True)
    picked = jnp.minimum(arrived, row_count - 1)
    where_from = (
        jnp.zeros((row_count,), jnp.int32)
        .at[arrived]
        .set(jnp.arange(buffer_rows, dtype=jnp.int32), mode="drop")
    )

    def place(pieces):
        return pieces[where_from]

    received = (
        lax.all_to_all(send_q, "seq", split_axis=0, concat_axis=0, tiled=True),
        lax.all_to_all(send_k, "seq", split_axis=0, concat_axis=0, tiled=True),
        lax.all_to_all(send_v, "seq", split_axis=0, concat_axis=0, tiled=True),
    )
    result = attend_local(place(received[0]), place(received[1]), place(received[2]))
    returned = lax.all_to_all(result[picked], "seq", split_axis=0, concat_axis=0, tiled=True)
    mixed = returned[send_row].reshape(row_count, heads_here * DH)
    return project_scatter(mixed, out_weight)


def swap_pairs(count, bit):
    return [(index, index ^ bit) for index in range(count)]


def project_scatter(mixed, out_weight):
    head_count = lax.axis_size("head")
    me = lax.axis_index("head")
    partner = me ^ 1
    width = out_weight.shape[1] // head_count

    def block(index):
        return lax.dynamic_slice_in_dim(out_weight, index * width, width, axis=1)

    def dot(weight):
        return jnp.dot(
            mixed, weight, precision=lax.Precision.HIGH, preferred_element_type=jnp.float32
        )

    for_partner_far = lax.ppermute(dot(block(partner ^ 2)), "head", swap_pairs(head_count, 1))
    far_sum = dot(block(me ^ 2)) + for_partner_far
    from_far = lax.ppermute(far_sum, "head", swap_pairs(head_count, 2))
    for_partner_near = lax.ppermute(dot(block(partner)), "head", swap_pairs(head_count, 1))
    near_sum = dot(block(me)) + for_partner_near
    return near_sum + from_far


def solution(mesh):
    in_specs = (
        P("seq", "head"),
        P("seq", "head"),
        P("seq", "head"),
        P("seq"),
        P("seq"),
        P("seq"),
        P("head", None),
    )
    out_specs = P("seq", "head")
    return jax.shard_map(
        per_device, mesh=mesh, in_specs=in_specs, out_specs=out_specs, check_vma=False
    )
```

```python
import math

import jax
import jax.numpy as jnp
from jax import lax
from jax.sharding import PartitionSpec as P

DH = 128
CS = 1024
CL_DEV = 1


ROPE_BASE = 500000.0
ORIG_CONTEXT = 8192.0
STRETCH = 4.0
BETA_FAST = 32.0
BETA_SLOW = 1.0


def yarn_tables(token_pos, width):
    half_width = width // 2
    expo = jnp.arange(half_width, dtype=jnp.float32) * 2.0 / width
    theta = jnp.exp(-expo * math.log(ROPE_BASE))
    ratio = ORIG_CONTEXT * theta / (2.0 * math.pi)
    ramp = jnp.clip((ratio - BETA_SLOW) / (BETA_FAST - BETA_SLOW), 0.0, 1.0)
    freq = theta * (ramp + (1.0 - ramp) / STRETCH)
    angle = token_pos.astype(jnp.float32)[:, None] * freq[None, :]
    mscale = 0.1 * math.log(STRETCH) + 1.0
    cos_table = jnp.concatenate([jnp.cos(angle), jnp.cos(angle)], -1) * mscale
    sin_table = jnp.concatenate([jnp.sin(angle), jnp.sin(angle)], -1) * mscale
    return (cos_table[:, None, :], sin_table[:, None, :])


def rotate(field, cos_table, sin_table):
    half_width = field.shape[-1] // 2
    turned = jnp.concatenate([-field[..., half_width:], field[..., :half_width]], -1)
    return field * cos_table + turned * sin_table


def cluster_attention(triple):
    query_c, key_c, value_c = triple
    length = query_c.shape[0]
    scores = jnp.einsum(
        "qhd,khd->hqk", query_c, key_c, precision=lax.Precision.HIGH
    ) / math.sqrt(query_c.shape[-1])
    causal = jnp.arange(length)[:, None] >= jnp.arange(length)[None, :]
    scores = jnp.where(causal[None], scores, -jnp.inf)
    peak = jnp.max(scores, -1, keepdims=True)
    weights = jnp.exp(scores - peak)
    total = jnp.sum(weights, -1, keepdims=True)
    summed = jnp.einsum("hqk,khd->qhd", weights, value_c, precision=lax.Precision.HIGH)
    return summed / jnp.transpose(total, (1, 0, 2))


def attend_local(query_all, key_all, value_all):
    row_count, head_count, width = query_all.shape
    grouped = (
        query_all.reshape(row_count // CS, CS, head_count, width),
        key_all.reshape(row_count // CS, CS, head_count, width),
        value_all.reshape(row_count // CS, CS, head_count, width),
    )
    return lax.map(cluster_attention, grouped).reshape(row_count, head_count, width)


def per_device(queries, keys, values, positions, cluster, slot, out_weight):
    seq_count = lax.axis_size("seq")
    row_count = queries.shape[0]
    capacity = 3 * row_count // (2 * seq_count)
    buffer_rows = seq_count * capacity
    heads_here = queries.shape[1] // DH
    owner_ids = cluster // CL_DEV
    target_row = cluster % CL_DEV * CS + slot
    one_hot = (owner_ids[:, None] == jnp.arange(seq_count)[None, :]).astype(jnp.int32)
    token_rank = jnp.sum(jnp.cumsum(one_hot, 0) * one_hot, 1) - 1
    send_row = owner_ids * capacity + token_rank
    source_token = (
        jnp.full((buffer_rows,), row_count, jnp.int32)
        .at[send_row]
        .set(jnp.arange(row_count, dtype=jnp.int32))
    )
    cos_table, sin_table = yarn_tables(positions, DH)
    shaped = (row_count, heads_here, DH)
    rot_q = rotate(queries.reshape(shaped), cos_table, sin_table)
    rot_k = rotate(keys.reshape(shaped), cos_table, sin_table)
    stacked = jnp.concatenate([rot_q, rot_k, values.reshape(shaped)], 1)
    stacked = jnp.concatenate([stacked, jnp.zeros((1, 3 * heads_here, DH), jnp.float32)], 0)
    send_all = stacked[source_token]
    send_q = send_all[:, :heads_here]
    send_k = send_all[:, heads_here : 2 * heads_here]
    send_v = send_all[:, 2 * heads_here :]
    slot_rows = jnp.full((buffer_rows,), row_count, jnp.int32).at[send_row].set(target_row)
    arrived = lax.all_to_all(slot_rows, "seq", split_axis=0, concat_axis=0, tiled=True)
    picked = jnp.minimum(arrived, row_count - 1)
    where_from = (
        jnp.zeros((row_count,), jnp.int32)
        .at[arrived]
        .set(jnp.arange(buffer_rows, dtype=jnp.int32), mode="drop")
    )

    def place(pieces):
        return pieces[where_from]

    far_weights = fetch_far_weights(out_weight)
    first_arrived = lax.all_to_all(send_q, "seq", split_axis=0, concat_axis=0, tiled=True)
    first_arrived, far_weights = lax.optimization_barrier((first_arrived, far_weights))
    received = (
        first_arrived,
        lax.all_to_all(send_k, "seq", split_axis=0, concat_axis=0, tiled=True),
        lax.all_to_all(send_v, "seq", split_axis=0, concat_axis=0, tiled=True),
    )
    result = attend_local(place(received[0]), place(received[1]), place(received[2]))
    returned = lax.all_to_all(result[picked], "seq", split_axis=0, concat_axis=0, tiled=True)
    mixed = returned[send_row].reshape(row_count, heads_here * DH)
    return project_scatter(mixed, out_weight, far_weights)


def swap_pairs(count, bit):
    return [(index, index ^ bit) for index in range(count)]


def weight_block(out_weight, index):
    width = out_weight.shape[1] // lax.axis_size("head")
    return lax.dynamic_slice_in_dim(out_weight, index * width, width, axis=1)


def fetch_far_weights(out_weight):
    head_count = lax.axis_size("head")
    me = lax.axis_index("head")
    outgoing = jnp.stack(
        [weight_block(out_weight, me ^ 2), weight_block(out_weight, me ^ 3)], 0
    )
    return lax.ppermute(outgoing, "head", swap_pairs(head_count, 2))


def project_scatter(mixed, out_weight, far_weights):
    head_count = lax.axis_size("head")
    me = lax.axis_index("head")

    def dot(lhs, weight):
        return jnp.dot(
            lhs, weight, precision=lax.Precision.HIGH, preferred_element_type=jnp.float32
        )

    far_mixed = lax.ppermute(mixed, "head", swap_pairs(head_count, 2))
    near_partner = dot(mixed, weight_block(out_weight, me ^ 1))
    for_partner = near_partner + dot(far_mixed, far_weights[1])
    from_partner = lax.ppermute(for_partner, "head", swap_pairs(head_count, 1))
    own = dot(mixed, weight_block(out_weight, me)) + dot(far_mixed, far_weights[0])
    return own + from_partner


def solution(mesh):
    in_specs = (
        P("seq", "head"),
        P("seq", "head"),
        P("seq", "head"),
        P("seq"),
        P("seq"),
        P("seq"),
        P("head", None),
    )
    out_specs = P("seq", "head")
    return jax.shard_map(
        per_device, mesh=mesh, in_specs=in_specs, out_specs=out_specs, check_vma=False
    )
```

```python
import math

import jax
import jax.numpy as jnp
from jax import lax
from jax.sharding import PartitionSpec as P

DH = 128
CS = 1024
CL_DEV = 1


ROPE_BASE = 500000.0
ORIG_CONTEXT = 8192.0
STRETCH = 4.0
BETA_FAST = 32.0
BETA_SLOW = 1.0


def yarn_tables(token_pos, width):
    half_width = width // 2
    expo = jnp.arange(half_width, dtype=jnp.float32) * 2.0 / width
    theta = jnp.exp(-expo * math.log(ROPE_BASE))
    ratio = ORIG_CONTEXT * theta / (2.0 * math.pi)
    ramp = jnp.clip((ratio - BETA_SLOW) / (BETA_FAST - BETA_SLOW), 0.0, 1.0)
    freq = theta * (ramp + (1.0 - ramp) / STRETCH)
    angle = token_pos.astype(jnp.float32)[:, None] * freq[None, :]
    mscale = 0.1 * math.log(STRETCH) + 1.0
    cos_table = jnp.concatenate([jnp.cos(angle), jnp.cos(angle)], -1) * mscale
    sin_table = jnp.concatenate([jnp.sin(angle), jnp.sin(angle)], -1) * mscale
    return (cos_table[:, None, :], sin_table[:, None, :])


def rotate(field, cos_table, sin_table):
    half_width = field.shape[-1] // 2
    turned = jnp.concatenate([-field[..., half_width:], field[..., :half_width]], -1)
    return field * cos_table + turned * sin_table


def cluster_attention(triple):
    query_c, key_c, value_c = triple
    length = query_c.shape[0]
    scores = jnp.einsum(
        "qhd,khd->hqk", query_c, key_c, precision=lax.Precision.HIGH
    ) / math.sqrt(query_c.shape[-1])
    causal = jnp.arange(length)[:, None] >= jnp.arange(length)[None, :]
    scores = jnp.where(causal[None], scores, -jnp.inf)
    peak = jnp.max(scores, -1, keepdims=True)
    weights = jnp.exp(scores - peak)
    total = jnp.sum(weights, -1, keepdims=True)
    summed = jnp.einsum("hqk,khd->qhd", weights, value_c, precision=lax.Precision.HIGH)
    return summed / jnp.transpose(total, (1, 0, 2))


def attend_local(query_all, key_all, value_all):
    row_count, head_count, width = query_all.shape
    grouped = (
        query_all.reshape(row_count // CS, CS, head_count, width),
        key_all.reshape(row_count // CS, CS, head_count, width),
        value_all.reshape(row_count // CS, CS, head_count, width),
    )
    return lax.map(cluster_attention, grouped).reshape(row_count, head_count, width)


def per_device(queries, keys, values, positions, cluster, slot, out_weight):
    seq_count = lax.axis_size("seq")
    row_count = queries.shape[0]
    capacity = 3 * row_count // (2 * seq_count)
    buffer_rows = seq_count * capacity
    heads_here = queries.shape[1] // DH
    owner_ids = cluster // CL_DEV
    target_row = cluster % CL_DEV * CS + slot
    one_hot = (owner_ids[:, None] == jnp.arange(seq_count)[None, :]).astype(jnp.int32)
    token_rank = jnp.sum(jnp.cumsum(one_hot, 0) * one_hot, 1) - 1
    send_row = owner_ids * capacity + token_rank
    source_token = (
        jnp.full((buffer_rows,), row_count, jnp.int32)
        .at[send_row]
        .set(jnp.arange(row_count, dtype=jnp.int32))
    )
    cos_table, sin_table = yarn_tables(positions, DH)
    shaped = (row_count, heads_here, DH)
    rot_q = rotate(queries.reshape(shaped), cos_table, sin_table)
    rot_k = rotate(keys.reshape(shaped), cos_table, sin_table)
    send_from = jnp.minimum(source_token, row_count - 1)
    send_q = rot_q[send_from]
    send_k = rot_k[send_from]
    send_v = values.reshape(shaped)[send_from]
    slot_rows = jnp.full((buffer_rows,), row_count, jnp.int32).at[send_row].set(target_row)
    arrived = lax.all_to_all(slot_rows, "seq", split_axis=0, concat_axis=0, tiled=True)
    picked = jnp.minimum(arrived, row_count - 1)
    where_from = (
        jnp.zeros((row_count,), jnp.int32)
        .at[arrived]
        .set(jnp.arange(buffer_rows, dtype=jnp.int32), mode="drop")
    )

    def place(pieces):
        return pieces[where_from]

    far_weights = fetch_far_weights(out_weight)
    first_arrived = lax.all_to_all(send_q, "seq", split_axis=0, concat_axis=0, tiled=True)
    first_arrived, far_weights = lax.optimization_barrier((first_arrived, far_weights))
    received = (
        first_arrived,
        lax.all_to_all(send_k, "seq", split_axis=0, concat_axis=0, tiled=True),
        lax.all_to_all(send_v, "seq", split_axis=0, concat_axis=0, tiled=True),
    )
    result = attend_local(place(received[0]), place(received[1]), place(received[2]))
    outgoing = result[picked]
    split = heads_here // 2
    mixed_parts = []
    for lo, hi in ((0, split), (split, heads_here)):
        back = lax.all_to_all(outgoing[:, lo:hi], "seq", split_axis=0, concat_axis=0, tiled=True)
        mixed_parts.append((back[send_row].reshape(row_count, (hi - lo) * DH), lo * DH, hi * DH))
    return project_scatter(mixed_parts, out_weight, far_weights)


def swap_pairs(count, bit):
    return [(index, index ^ bit) for index in range(count)]


def weight_block(out_weight, index):
    width = out_weight.shape[1] // lax.axis_size("head")
    return lax.dynamic_slice_in_dim(out_weight, index * width, width, axis=1)


def fetch_far_weights(out_weight):
    head_count = lax.axis_size("head")
    me = lax.axis_index("head")
    outgoing = jnp.stack(
        [weight_block(out_weight, me ^ 2), weight_block(out_weight, me ^ 3)], 0
    )
    return lax.ppermute(outgoing, "head", swap_pairs(head_count, 2))


def project_scatter(mixed_parts, out_weight, far_weights):
    head_count = lax.axis_size("head")
    me = lax.axis_index("head")
    partner_w = weight_block(out_weight, me ^ 1)
    own_w = weight_block(out_weight, me)

    def dot(lhs, weight):
        return jnp.dot(
            lhs, weight, precision=lax.Precision.HIGH, preferred_element_type=jnp.float32
        )

    for_partner = 0.0
    own = 0.0
    for mixed, lo, hi in mixed_parts:
        far_mixed = lax.ppermute(mixed, "head", swap_pairs(head_count, 2))
        for_partner = for_partner + dot(mixed, partner_w[lo:hi])
        for_partner = for_partner + dot(far_mixed, far_weights[1, lo:hi])
        own = own + dot(mixed, own_w[lo:hi]) + dot(far_mixed, far_weights[0, lo:hi])
    from_partner = lax.ppermute(for_partner, "head", swap_pairs(head_count, 1))
    return own + from_partner


def solution(mesh):
    in_specs = (
        P("seq", "head"),
        P("seq", "head"),
        P("seq", "head"),
        P("seq"),
        P("seq"),
        P("seq"),
        P("head", None),
    )
    out_specs = P("seq", "head")
    return jax.shard_map(
        per_device, mesh=mesh, in_specs=in_specs, out_specs=out_specs, check_vma=False
    )
```

```python
import math

import jax
import jax.numpy as jnp
from jax import lax
from jax.sharding import PartitionSpec as P

DH = 128
CS = 1024
CL_DEV = 1


ROPE_BASE = 500000.0
ORIG_CONTEXT = 8192.0
STRETCH = 4.0
BETA_FAST = 32.0
BETA_SLOW = 1.0


def yarn_tables(token_pos, width):
    half_width = width // 2
    expo = jnp.arange(half_width, dtype=jnp.float32) * 2.0 / width
    theta = jnp.exp(-expo * math.log(ROPE_BASE))
    ratio = ORIG_CONTEXT * theta / (2.0 * math.pi)
    ramp = jnp.clip((ratio - BETA_SLOW) / (BETA_FAST - BETA_SLOW), 0.0, 1.0)
    freq = theta * (ramp + (1.0 - ramp) / STRETCH)
    angle = token_pos.astype(jnp.float32)[:, None] * freq[None, :]
    mscale = 0.1 * math.log(STRETCH) + 1.0
    cos_table = jnp.concatenate([jnp.cos(angle), jnp.cos(angle)], -1) * mscale
    sin_table = jnp.concatenate([jnp.sin(angle), jnp.sin(angle)], -1) * mscale
    return (cos_table[:, None, :], sin_table[:, None, :])


def rotate(field, cos_table, sin_table):
    half_width = field.shape[-1] // 2
    turned = jnp.concatenate([-field[..., half_width:], field[..., :half_width]], -1)
    return field * cos_table + turned * sin_table


def cluster_attention(triple):
    query_c, key_c, value_c = triple
    length = query_c.shape[0]
    scores = jnp.einsum(
        "qhd,khd->hqk", query_c, key_c, precision=lax.Precision.HIGH
    ) / math.sqrt(query_c.shape[-1])
    causal = jnp.arange(length)[:, None] >= jnp.arange(length)[None, :]
    scores = jnp.where(causal[None], scores, -jnp.inf)
    peak = jnp.max(scores, -1, keepdims=True)
    weights = jnp.exp(scores - peak)
    total = jnp.sum(weights, -1, keepdims=True)
    summed = jnp.einsum("hqk,khd->qhd", weights, value_c, precision=lax.Precision.HIGH)
    return summed / jnp.transpose(total, (1, 0, 2))


def attend_local(query_all, key_all, value_all):
    row_count, head_count, width = query_all.shape
    grouped = (
        query_all.reshape(row_count // CS, CS, head_count, width),
        key_all.reshape(row_count // CS, CS, head_count, width),
        value_all.reshape(row_count // CS, CS, head_count, width),
    )
    return lax.map(cluster_attention, grouped).reshape(row_count, head_count, width)


def per_device(queries, keys, values, positions, cluster, slot, out_weight):
    seq_count = lax.axis_size("seq")
    row_count = queries.shape[0]
    capacity = 3 * row_count // (2 * seq_count)
    buffer_rows = seq_count * capacity
    heads_here = queries.shape[1] // DH
    owner_ids = cluster // CL_DEV
    target_row = cluster % CL_DEV * CS + slot
    one_hot = (owner_ids[:, None] == jnp.arange(seq_count)[None, :]).astype(jnp.int32)
    token_rank = jnp.sum(jnp.cumsum(one_hot, 0) * one_hot, 1) - 1
    send_row = owner_ids * capacity + token_rank
    source_token = (
        jnp.full((buffer_rows,), row_count, jnp.int32)
        .at[send_row]
        .set(jnp.arange(row_count, dtype=jnp.int32))
    )
    cos_table, sin_table = yarn_tables(positions, DH)
    shaped = (row_count, heads_here, DH)
    rot_q = rotate(queries.reshape(shaped), cos_table, sin_table)
    rot_k = rotate(keys.reshape(shaped), cos_table, sin_table)
    send_from = jnp.minimum(source_token, row_count - 1)
    send_q = rot_q[send_from]
    send_k = rot_k[send_from]
    send_v = values.reshape(shaped)[send_from]
    slot_rows = jnp.full((buffer_rows,), row_count, jnp.int32).at[send_row].set(target_row)
    arrived = lax.all_to_all(slot_rows, "seq", split_axis=0, concat_axis=0, tiled=True)
    picked = jnp.minimum(arrived, row_count - 1)
    where_from = (
        jnp.zeros((row_count,), jnp.int32)
        .at[arrived]
        .set(jnp.arange(buffer_rows, dtype=jnp.int32), mode="drop")
    )

    def place(pieces):
        return pieces[where_from]

    far_weights = fetch_far_weights(out_weight)
    arrived_v = lax.all_to_all(send_v, "seq", split_axis=0, concat_axis=0, tiled=True)
    arrived_v, far_weights = lax.optimization_barrier((arrived_v, far_weights))
    arrived_q = lax.all_to_all(send_q, "seq", split_axis=0, concat_axis=0, tiled=True)
    arrived_k = lax.all_to_all(send_k, "seq", split_axis=0, concat_axis=0, tiled=True)
    placed = (place(arrived_q), place(arrived_k), place(arrived_v))
    split = heads_here // 2
    mixed_parts = []
    for lo, hi in ((0, split), (split, heads_here)):
        result = attend_local(*(piece[:, lo:hi] for piece in placed))
        back = lax.all_to_all(result[picked], "seq", split_axis=0, concat_axis=0, tiled=True)
        mixed_parts.append((back[send_row].reshape(row_count, (hi - lo) * DH), lo * DH, hi * DH))
    return project_scatter(mixed_parts, out_weight, far_weights)


def swap_pairs(count, bit):
    return [(index, index ^ bit) for index in range(count)]


def weight_block(out_weight, index):
    width = out_weight.shape[1] // lax.axis_size("head")
    return lax.dynamic_slice_in_dim(out_weight, index * width, width, axis=1)


def fetch_far_weights(out_weight):
    head_count = lax.axis_size("head")
    me = lax.axis_index("head")
    outgoing = jnp.stack(
        [weight_block(out_weight, me ^ 2), weight_block(out_weight, me ^ 3)], 0
    )
    return lax.ppermute(outgoing, "head", swap_pairs(head_count, 2))


def project_scatter(mixed_parts, out_weight, far_weights):
    head_count = lax.axis_size("head")
    me = lax.axis_index("head")
    partner_w = weight_block(out_weight, me ^ 1)
    own_w = weight_block(out_weight, me)

    def dot(lhs, weight):
        return jnp.dot(
            lhs, weight, precision=lax.Precision.HIGH, preferred_element_type=jnp.float32
        )

    terms_partner = []
    terms_own = []
    for mixed, lo, hi in mixed_parts:
        far_mixed = lax.ppermute(mixed, "head", swap_pairs(head_count, 2))
        terms_partner += [(mixed, partner_w[lo:hi]), (far_mixed, far_weights[1, lo:hi])]
        terms_own += [(mixed, own_w[lo:hi]), (far_mixed, far_weights[0, lo:hi])]
    for_partner = dot(*terms_partner[0])
    for term in terms_partner[1:]:
        for_partner = for_partner + dot(*term)
    from_partner = lax.ppermute(for_partner, "head", swap_pairs(head_count, 1))
    own = dot(*terms_own[0])
    for term in terms_own[1:]:
        own = own + dot(*term)
    return own + from_partner


def solution(mesh):
    in_specs = (
        P("seq", "head"),
        P("seq", "head"),
        P("seq", "head"),
        P("seq"),
        P("seq"),
        P("seq"),
        P("head", None),
    )
    out_specs = P("seq", "head")
    return jax.shard_map(
        per_device, mesh=mesh, in_specs=in_specs, out_specs=out_specs, check_vma=False
    )
```

```python
import math

import jax
import jax.numpy as jnp
from jax import lax
from jax.sharding import PartitionSpec as P

DH = 128
CS = 1024
CL_DEV = 1


ROPE_BASE = 500000.0
ORIG_CONTEXT = 8192.0
STRETCH = 4.0
BETA_FAST = 32.0
BETA_SLOW = 1.0


def yarn_tables(token_pos, width):
    half_width = width // 2
    expo = jnp.arange(half_width, dtype=jnp.float32) * 2.0 / width
    theta = jnp.exp(-expo * math.log(ROPE_BASE))
    ratio = ORIG_CONTEXT * theta / (2.0 * math.pi)
    ramp = jnp.clip((ratio - BETA_SLOW) / (BETA_FAST - BETA_SLOW), 0.0, 1.0)
    freq = theta * (ramp + (1.0 - ramp) / STRETCH)
    angle = token_pos.astype(jnp.float32)[:, None] * freq[None, :]
    mscale = 0.1 * math.log(STRETCH) + 1.0
    cos_table = jnp.concatenate([jnp.cos(angle), jnp.cos(angle)], -1) * mscale
    sin_table = jnp.concatenate([jnp.sin(angle), jnp.sin(angle)], -1) * mscale
    return (cos_table[:, None, :], sin_table[:, None, :])


def rotate(field, cos_table, sin_table):
    half_width = field.shape[-1] // 2
    turned = jnp.concatenate([-field[..., half_width:], field[..., :half_width]], -1)
    return field * cos_table + turned * sin_table


def cluster_attention(triple):
    query_c, key_c, value_c = triple
    length = query_c.shape[0]
    scores = jnp.einsum(
        "qhd,khd->hqk", query_c, key_c, precision=lax.Precision.HIGH
    ) / math.sqrt(query_c.shape[-1])
    causal = jnp.arange(length)[:, None] >= jnp.arange(length)[None, :]
    scores = jnp.where(causal[None], scores, -jnp.inf)
    peak = jnp.max(scores, -1, keepdims=True)
    weights = jnp.exp(scores - peak)
    total = jnp.sum(weights, -1, keepdims=True)
    summed = jnp.einsum("hqk,khd->qhd", weights, value_c, precision=lax.Precision.HIGH)
    return summed / jnp.transpose(total, (1, 0, 2))


def attend_local(query_all, key_all, value_all):
    row_count, head_count, width = query_all.shape
    grouped = (
        query_all.reshape(row_count // CS, CS, head_count, width),
        key_all.reshape(row_count // CS, CS, head_count, width),
        value_all.reshape(row_count // CS, CS, head_count, width),
    )
    return lax.map(cluster_attention, grouped).reshape(row_count, head_count, width)


def per_device(queries, keys, values, positions, cluster, slot, out_weight):
    seq_count = lax.axis_size("seq")
    row_count = queries.shape[0]
    capacity = 3 * row_count // (2 * seq_count)
    buffer_rows = seq_count * capacity
    heads_here = queries.shape[1] // DH
    owner_ids = cluster // CL_DEV
    target_row = cluster % CL_DEV * CS + slot
    one_hot = (owner_ids[:, None] == jnp.arange(seq_count)[None, :]).astype(jnp.int32)
    token_rank = jnp.sum(jnp.cumsum(one_hot, 0) * one_hot, 1) - 1
    send_row = owner_ids * capacity + token_rank
    source_token = (
        jnp.full((buffer_rows,), row_count, jnp.int32)
        .at[send_row]
        .set(jnp.arange(row_count, dtype=jnp.int32))
    )
    cos_table, sin_table = yarn_tables(positions, DH)
    shaped = (row_count, heads_here, DH)
    rot_q = rotate(queries.reshape(shaped), cos_table, sin_table)
    rot_k = rotate(keys.reshape(shaped), cos_table, sin_table)
    send_from = jnp.minimum(source_token, row_count - 1)
    send_q = rot_q[send_from]
    send_k = rot_k[send_from]
    send_v = values.reshape(shaped)[send_from]
    slot_rows = jnp.full((buffer_rows,), row_count, jnp.int32).at[send_row].set(target_row)
    arrived = lax.all_to_all(slot_rows, "seq", split_axis=0, concat_axis=0, tiled=True)
    picked = jnp.minimum(arrived, row_count - 1)
    where_from = (
        jnp.zeros((row_count,), jnp.int32)
        .at[arrived]
        .set(jnp.arange(buffer_rows, dtype=jnp.int32), mode="drop")
    )

    def place(pieces):
        return pieces[where_from]

    far_weights = fetch_far_weights(out_weight)
    arrived_q = lax.all_to_all(send_q, "seq", split_axis=0, concat_axis=0, tiled=True)
    send_k, far_weights = lax.optimization_barrier((send_k, far_weights))
    arrived_k = lax.all_to_all(send_k, "seq", split_axis=0, concat_axis=0, tiled=True)
    arrived_v = lax.all_to_all(send_v, "seq", split_axis=0, concat_axis=0, tiled=True)
    placed = (place(arrived_q), place(arrived_k), place(arrived_v))
    split = heads_here // 2
    mixed_parts = []
    for lo, hi in ((0, split), (split, heads_here)):
        result = attend_local(*(piece[:, lo:hi] for piece in placed))
        back = lax.all_to_all(result[picked], "seq", split_axis=0, concat_axis=0, tiled=True)
        mixed_parts.append((back[send_row].reshape(row_count, (hi - lo) * DH), lo * DH, hi * DH))
    return project_scatter(mixed_parts, out_weight, far_weights)


def swap_pairs(count, bit):
    return [(index, index ^ bit) for index in range(count)]


def weight_block(out_weight, index):
    width = out_weight.shape[1] // lax.axis_size("head")
    return lax.dynamic_slice_in_dim(out_weight, index * width, width, axis=1)


def fetch_far_weights(out_weight):
    head_count = lax.axis_size("head")
    me = lax.axis_index("head")
    outgoing = jnp.stack(
        [weight_block(out_weight, me ^ 2), weight_block(out_weight, me ^ 3)], 0
    )
    return lax.ppermute(outgoing, "head", swap_pairs(head_count, 2))


def project_scatter(mixed_parts, out_weight, far_weights):
    head_count = lax.axis_size("head")
    me = lax.axis_index("head")
    partner_w = weight_block(out_weight, me ^ 1)
    own_w = weight_block(out_weight, me)

    def dot(lhs, weight):
        return jnp.dot(
            lhs, weight, precision=lax.Precision.HIGH, preferred_element_type=jnp.float32
        )

    terms_partner = []
    terms_own = []
    for mixed, lo, hi in mixed_parts:
        far_mixed = lax.ppermute(mixed, "head", swap_pairs(head_count, 2))
        terms_partner += [(mixed, partner_w[lo:hi]), (far_mixed, far_weights[1, lo:hi])]
        terms_own += [(mixed, own_w[lo:hi]), (far_mixed, far_weights[0, lo:hi])]
    for_partner = dot(*terms_partner[0])
    for term in terms_partner[1:]:
        for_partner = for_partner + dot(*term)
    from_partner = lax.ppermute(for_partner, "head", swap_pairs(head_count, 1))
    own = dot(*terms_own[0])
    for term in terms_own[1:]:
        own = own + dot(*term)
    return own + from_partner


def solution(mesh):
    in_specs = (
        P("seq", "head"),
        P("seq", "head"),
        P("seq", "head"),
        P("seq"),
        P("seq"),
        P("seq"),
        P("head", None),
    )
    out_specs = P("seq", "head")
    return jax.shard_map(
        per_device, mesh=mesh, in_specs=in_specs, out_specs=out_specs, check_vma=False
    )
```

```python
import math

import jax
import jax.numpy as jnp
from jax import lax
from jax.sharding import PartitionSpec as P

DH = 128
CS = 1024
CL_DEV = 1


ROPE_BASE = 500000.0
ORIG_CONTEXT = 8192.0
STRETCH = 4.0
BETA_FAST = 32.0
BETA_SLOW = 1.0


def yarn_tables(token_pos, width):
    half_width = width // 2
    expo = jnp.arange(half_width, dtype=jnp.float32) * 2.0 / width
    theta = jnp.exp(-expo * math.log(ROPE_BASE))
    ratio = ORIG_CONTEXT * theta / (2.0 * math.pi)
    ramp = jnp.clip((ratio - BETA_SLOW) / (BETA_FAST - BETA_SLOW), 0.0, 1.0)
    freq = theta * (ramp + (1.0 - ramp) / STRETCH)
    angle = token_pos.astype(jnp.float32)[:, None] * freq[None, :]
    mscale = 0.1 * math.log(STRETCH) + 1.0
    cos_table = jnp.concatenate([jnp.cos(angle), jnp.cos(angle)], -1) * mscale
    sin_table = jnp.concatenate([jnp.sin(angle), jnp.sin(angle)], -1) * mscale
    return (cos_table[:, None, :], sin_table[:, None, :])


def rotate(field, cos_table, sin_table):
    half_width = field.shape[-1] // 2
    turned = jnp.concatenate([-field[..., half_width:], field[..., :half_width]], -1)
    return field * cos_table + turned * sin_table


def cluster_attention(triple):
    query_c, key_c, value_c = triple
    length = query_c.shape[0]
    scores = jnp.einsum(
        "qhd,khd->hqk", query_c, key_c, precision=lax.Precision.HIGH
    ) / math.sqrt(query_c.shape[-1])
    causal = jnp.arange(length)[:, None] >= jnp.arange(length)[None, :]
    scores = jnp.where(causal[None], scores, -jnp.inf)
    peak = jnp.max(scores, -1, keepdims=True)
    weights = jnp.exp(scores - peak)
    total = jnp.sum(weights, -1, keepdims=True)
    summed = jnp.einsum("hqk,khd->qhd", weights, value_c, precision=lax.Precision.HIGH)
    return summed / jnp.transpose(total, (1, 0, 2))


def attend_local(query_all, key_all, value_all):
    row_count, head_count, width = query_all.shape
    grouped = (
        query_all.reshape(row_count // CS, CS, head_count, width),
        key_all.reshape(row_count // CS, CS, head_count, width),
        value_all.reshape(row_count // CS, CS, head_count, width),
    )
    return lax.map(cluster_attention, grouped).reshape(row_count, head_count, width)


def per_device(queries, keys, values, positions, cluster, slot, out_weight):
    seq_count = lax.axis_size("seq")
    row_count = queries.shape[0]
    capacity = 3 * row_count // (2 * seq_count)
    buffer_rows = seq_count * capacity
    heads_here = queries.shape[1] // DH
    owner_ids = cluster // CL_DEV
    target_row = cluster % CL_DEV * CS + slot
    one_hot = (owner_ids[:, None] == jnp.arange(seq_count)[None, :]).astype(jnp.int32)
    token_rank = jnp.sum(jnp.cumsum(one_hot, 0) * one_hot, 1) - 1
    send_row = owner_ids * capacity + token_rank
    source_token = (
        jnp.full((buffer_rows,), row_count, jnp.int32)
        .at[send_row]
        .set(jnp.arange(row_count, dtype=jnp.int32))
    )
    cos_table, sin_table = yarn_tables(positions, DH)
    shaped = (row_count, heads_here, DH)
    rot_q = rotate(queries.reshape(shaped), cos_table, sin_table)
    rot_k = rotate(keys.reshape(shaped), cos_table, sin_table)
    send_from = jnp.minimum(source_token, row_count - 1)
    send_q = rot_q[send_from]
    send_k = rot_k[send_from]
    send_v = values.reshape(shaped)[send_from]
    slot_rows = jnp.full((buffer_rows,), row_count, jnp.int32).at[send_row].set(target_row)
    arrived = lax.all_to_all(slot_rows, "seq", split_axis=0, concat_axis=0, tiled=True)
    picked = jnp.minimum(arrived, row_count - 1)
    where_from = (
        jnp.zeros((row_count,), jnp.int32)
        .at[arrived]
        .set(jnp.arange(buffer_rows, dtype=jnp.int32), mode="drop")
    )

    def place(pieces):
        return pieces[where_from]

    far_weights = fetch_far_weights(out_weight)
    far_own, far_partner = far_weights
    arrived_q = lax.all_to_all(send_q, "seq", split_axis=0, concat_axis=0, tiled=True)
    arrived_q, far_own = lax.optimization_barrier((arrived_q, far_own))
    send_k, far_partner = lax.optimization_barrier((send_k, far_partner))
    far_weights = (far_own, far_partner)
    arrived_k = lax.all_to_all(send_k, "seq", split_axis=0, concat_axis=0, tiled=True)
    arrived_v = lax.all_to_all(send_v, "seq", split_axis=0, concat_axis=0, tiled=True)
    placed = (place(arrived_q), place(arrived_k), place(arrived_v))
    split = heads_here // 2
    mixed_parts = []
    for lo, hi in ((0, split), (split, heads_here)):
        result = attend_local(*(piece[:, lo:hi] for piece in placed))
        back = lax.all_to_all(result[picked], "seq", split_axis=0, concat_axis=0, tiled=True)
        mixed_parts.append((back[send_row].reshape(row_count, (hi - lo) * DH), lo * DH, hi * DH))
    return project_scatter(mixed_parts, out_weight, far_weights)


def swap_pairs(count, bit):
    return [(index, index ^ bit) for index in range(count)]


def weight_block(out_weight, index):
    width = out_weight.shape[1] // lax.axis_size("head")
    return lax.dynamic_slice_in_dim(out_weight, index * width, width, axis=1)


def fetch_far_weights(out_weight):
    head_count = lax.axis_size("head")
    me = lax.axis_index("head")
    pairs = swap_pairs(head_count, 2)
    for_own = lax.ppermute(weight_block(out_weight, me ^ 2), "head", pairs)
    for_partner = lax.ppermute(weight_block(out_weight, me ^ 3), "head", pairs)
    return for_own, for_partner


def project_scatter(mixed_parts, out_weight, far_weights):
    head_count = lax.axis_size("head")
    me = lax.axis_index("head")
    partner_w = weight_block(out_weight, me ^ 1)
    own_w = weight_block(out_weight, me)

    def dot(lhs, weight):
        return jnp.dot(
            lhs, weight, precision=lax.Precision.HIGH, preferred_element_type=jnp.float32
        )

    terms_partner = []
    terms_own = []
    for mixed, lo, hi in mixed_parts:
        far_mixed = lax.ppermute(mixed, "head", swap_pairs(head_count, 2))
        terms_partner += [(mixed, partner_w[lo:hi]), (far_mixed, far_weights[1][lo:hi])]
        terms_own += [(mixed, own_w[lo:hi]), (far_mixed, far_weights[0][lo:hi])]
    for_partner = dot(*terms_partner[0])
    for term in terms_partner[1:]:
        for_partner = for_partner + dot(*term)
    from_partner = lax.ppermute(for_partner, "head", swap_pairs(head_count, 1))
    own = dot(*terms_own[0])
    for term in terms_own[1:]:
        own = own + dot(*term)
    return own + from_partner


def solution(mesh):
    in_specs = (
        P("seq", "head"),
        P("seq", "head"),
        P("seq", "head"),
        P("seq"),
        P("seq"),
        P("seq"),
        P("head", None),
    )
    out_specs = P("seq", "head")
    return jax.shard_map(
        per_device, mesh=mesh, in_specs=in_specs, out_specs=out_specs, check_vma=False
    )
```

```python
import math

import jax
import jax.numpy as jnp
from jax import lax
from jax.sharding import PartitionSpec as P

DH = 128
CS = 1024
CL_DEV = 1


ROPE_BASE = 500000.0
ORIG_CONTEXT = 8192.0
STRETCH = 4.0
BETA_FAST = 32.0
BETA_SLOW = 1.0


def yarn_tables(token_pos, width):
    half_width = width // 2
    expo = jnp.arange(half_width, dtype=jnp.float32) * 2.0 / width
    theta = jnp.exp(-expo * math.log(ROPE_BASE))
    ratio = ORIG_CONTEXT * theta / (2.0 * math.pi)
    ramp = jnp.clip((ratio - BETA_SLOW) / (BETA_FAST - BETA_SLOW), 0.0, 1.0)
    freq = theta * (ramp + (1.0 - ramp) / STRETCH)
    angle = token_pos.astype(jnp.float32)[:, None] * freq[None, :]
    mscale = 0.1 * math.log(STRETCH) + 1.0
    cos_table = jnp.concatenate([jnp.cos(angle), jnp.cos(angle)], -1) * mscale
    sin_table = jnp.concatenate([jnp.sin(angle), jnp.sin(angle)], -1) * mscale
    return (cos_table[:, None, :], sin_table[:, None, :])


def rotate(field, cos_table, sin_table):
    half_width = field.shape[-1] // 2
    turned = jnp.concatenate([-field[..., half_width:], field[..., :half_width]], -1)
    return field * cos_table + turned * sin_table


def cluster_attention(triple):
    query_c, key_c, value_c = triple
    length = query_c.shape[0]
    scores = jnp.einsum(
        "qhd,khd->hqk", query_c, key_c, precision=lax.Precision.HIGH
    ) / math.sqrt(query_c.shape[-1])
    causal = jnp.arange(length)[:, None] >= jnp.arange(length)[None, :]
    scores = jnp.where(causal[None], scores, -jnp.inf)
    peak = jnp.max(scores, -1, keepdims=True)
    weights = jnp.exp(scores - peak)
    total = jnp.sum(weights, -1, keepdims=True)
    summed = jnp.einsum("hqk,khd->qhd", weights, value_c, precision=lax.Precision.HIGH)
    return summed / jnp.transpose(total, (1, 0, 2))


def attend_local(query_all, key_all, value_all):
    row_count, head_count, width = query_all.shape
    grouped = (
        query_all.reshape(row_count // CS, CS, head_count, width),
        key_all.reshape(row_count // CS, CS, head_count, width),
        value_all.reshape(row_count // CS, CS, head_count, width),
    )
    return lax.map(cluster_attention, grouped).reshape(row_count, head_count, width)


def per_device(queries, keys, values, positions, cluster, slot, out_weight):
    seq_count = lax.axis_size("seq")
    row_count = queries.shape[0]
    capacity = 3 * row_count // (2 * seq_count)
    buffer_rows = seq_count * capacity
    heads_here = queries.shape[1] // DH
    owner_ids = cluster // CL_DEV
    target_row = cluster % CL_DEV * CS + slot
    one_hot = (owner_ids[:, None] == jnp.arange(seq_count)[None, :]).astype(jnp.int32)
    token_rank = jnp.sum(jnp.cumsum(one_hot, 0) * one_hot, 1) - 1
    send_row = owner_ids * capacity + token_rank
    source_token = (
        jnp.full((buffer_rows,), row_count, jnp.int32)
        .at[send_row]
        .set(jnp.arange(row_count, dtype=jnp.int32))
    )
    cos_table, sin_table = yarn_tables(positions, DH)
    shaped = (row_count, heads_here, DH)
    rot_q = rotate(queries.reshape(shaped), cos_table, sin_table)
    rot_k = rotate(keys.reshape(shaped), cos_table, sin_table)
    send_from = jnp.minimum(source_token, row_count - 1)
    send_q = rot_q[send_from]
    send_k = rot_k[send_from]
    send_v = values.reshape(shaped)[send_from]
    slot_rows = jnp.full((buffer_rows,), row_count, jnp.int32).at[send_row].set(target_row)
    arrived = lax.all_to_all(slot_rows, "seq", split_axis=0, concat_axis=0, tiled=True)
    picked = jnp.minimum(arrived, row_count - 1)
    where_from = (
        jnp.zeros((row_count,), jnp.int32)
        .at[arrived]
        .set(jnp.arange(buffer_rows, dtype=jnp.int32), mode="drop")
    )

    def place(pieces):
        return pieces[where_from]

    far_weights = fetch_far_weights(out_weight)
    first_arrived = lax.all_to_all(send_q, "seq", split_axis=0, concat_axis=0, tiled=True)
    first_arrived, far_weights = lax.optimization_barrier((first_arrived, far_weights))
    received = (
        first_arrived,
        lax.all_to_all(send_k, "seq", split_axis=0, concat_axis=0, tiled=True),
        lax.all_to_all(send_v, "seq", split_axis=0, concat_axis=0, tiled=True),
    )
    result = attend_local(place(received[0]), place(received[1]), place(received[2]))
    outgoing = result[picked]
    split = heads_here // 2
    head_count = lax.axis_size("head")
    me = lax.axis_index("head")
    partner_w = weight_block(out_weight, me ^ 1)
    own_w = weight_block(out_weight, me)

    def dot(lhs, weight):
        return jnp.dot(
            lhs, weight, precision=lax.Precision.HIGH, preferred_element_type=jnp.float32
        )

    def exchange(lo, hi):
        back = lax.all_to_all(outgoing[:, lo:hi], "seq", split_axis=0, concat_axis=0, tiled=True)
        return back

    def half_terms(back, lo, hi):
        mixed = back[send_row].reshape(row_count, (hi - lo) * DH)
        far_mixed = lax.ppermute(mixed, "head", swap_pairs(head_count, 2))
        rows = slice(lo * DH, hi * DH)
        to_partner = dot(mixed, partner_w[rows]) + dot(far_mixed, far_weights[1, rows])
        to_own = dot(mixed, own_w[rows]) + dot(far_mixed, far_weights[0, rows])
        return to_partner, to_own

    first_partner, first_own = half_terms(exchange(0, split), 0, split)
    second_back = exchange(split, heads_here)
    second_back, first_partner, first_own = lax.optimization_barrier(
        (second_back, first_partner, first_own)
    )
    second_partner, second_own = half_terms(second_back, split, heads_here)
    for_partner = first_partner + second_partner
    from_partner = lax.ppermute(for_partner, "head", swap_pairs(head_count, 1))
    return first_own + second_own + from_partner


def swap_pairs(count, bit):
    return [(index, index ^ bit) for index in range(count)]


def weight_block(out_weight, index):
    width = out_weight.shape[1] // lax.axis_size("head")
    return lax.dynamic_slice_in_dim(out_weight, index * width, width, axis=1)


def fetch_far_weights(out_weight):
    head_count = lax.axis_size("head")
    me = lax.axis_index("head")
    outgoing = jnp.stack(
        [weight_block(out_weight, me ^ 2), weight_block(out_weight, me ^ 3)], 0
    )
    return lax.ppermute(outgoing, "head", swap_pairs(head_count, 2))


def solution(mesh):
    in_specs = (
        P("seq", "head"),
        P("seq", "head"),
        P("seq", "head"),
        P("seq"),
        P("seq"),
        P("seq"),
        P("head", None),
    )
    out_specs = P("seq", "head")
    return jax.shard_map(
        per_device, mesh=mesh, in_specs=in_specs, out_specs=out_specs, check_vma=False
    )
```

```python
import math

import jax
import jax.numpy as jnp
from jax import lax
from jax.sharding import PartitionSpec as P

DH = 128
CS = 1024
CL_DEV = 1


ROPE_BASE = 500000.0
ORIG_CONTEXT = 8192.0
STRETCH = 4.0
BETA_FAST = 32.0
BETA_SLOW = 1.0


def yarn_tables(token_pos, width):
    half_width = width // 2
    expo = jnp.arange(half_width, dtype=jnp.float32) * 2.0 / width
    theta = jnp.exp(-expo * math.log(ROPE_BASE))
    ratio = ORIG_CONTEXT * theta / (2.0 * math.pi)
    ramp = jnp.clip((ratio - BETA_SLOW) / (BETA_FAST - BETA_SLOW), 0.0, 1.0)
    freq = theta * (ramp + (1.0 - ramp) / STRETCH)
    angle = token_pos.astype(jnp.float32)[:, None] * freq[None, :]
    mscale = 0.1 * math.log(STRETCH) + 1.0
    cos_table = jnp.concatenate([jnp.cos(angle), jnp.cos(angle)], -1) * mscale
    sin_table = jnp.concatenate([jnp.sin(angle), jnp.sin(angle)], -1) * mscale
    return (cos_table[:, None, :], sin_table[:, None, :])


def rotate(field, cos_table, sin_table):
    half_width = field.shape[-1] // 2
    turned = jnp.concatenate([-field[..., half_width:], field[..., :half_width]], -1)
    return field * cos_table + turned * sin_table


def cluster_attention(triple):
    query_c, key_c, value_c = triple
    length = query_c.shape[0]
    scores = jnp.einsum(
        "qhd,khd->hqk", query_c, key_c, precision=lax.Precision.HIGH
    ) / math.sqrt(query_c.shape[-1])
    causal = jnp.arange(length)[:, None] >= jnp.arange(length)[None, :]
    scores = jnp.where(causal[None], scores, -jnp.inf)
    peak = jnp.max(scores, -1, keepdims=True)
    weights = jnp.exp(scores - peak)
    total = jnp.sum(weights, -1, keepdims=True)
    summed = jnp.einsum("hqk,khd->qhd", weights, value_c, precision=lax.Precision.HIGH)
    return summed / jnp.transpose(total, (1, 0, 2))


def attend_local(query_all, key_all, value_all):
    row_count, head_count, width = query_all.shape
    grouped = (
        query_all.reshape(row_count // CS, CS, head_count, width),
        key_all.reshape(row_count // CS, CS, head_count, width),
        value_all.reshape(row_count // CS, CS, head_count, width),
    )
    return lax.map(cluster_attention, grouped).reshape(row_count, head_count, width)


def per_device(queries, keys, values, positions, cluster, slot, out_weight):
    seq_count = lax.axis_size("seq")
    row_count = queries.shape[0]
    capacity = 3 * row_count // (2 * seq_count)
    buffer_rows = seq_count * capacity
    heads_here = queries.shape[1] // DH
    owner_ids = cluster // CL_DEV
    target_row = cluster % CL_DEV * CS + slot
    one_hot = (owner_ids[:, None] == jnp.arange(seq_count)[None, :]).astype(jnp.int32)
    token_rank = jnp.sum(jnp.cumsum(one_hot, 0) * one_hot, 1) - 1
    send_row = owner_ids * capacity + token_rank
    source_token = (
        jnp.full((buffer_rows,), row_count, jnp.int32)
        .at[send_row]
        .set(jnp.arange(row_count, dtype=jnp.int32))
    )
    cos_table, sin_table = yarn_tables(positions, DH)
    shaped = (row_count, heads_here, DH)
    rot_q = rotate(queries.reshape(shaped), cos_table, sin_table)
    rot_k = rotate(keys.reshape(shaped), cos_table, sin_table)
    send_from = jnp.minimum(source_token, row_count - 1)
    send_q = rot_q[send_from]
    send_k = rot_k[send_from]
    send_v = values.reshape(shaped)[send_from]
    slot_rows = jnp.full((buffer_rows,), row_count, jnp.int32).at[send_row].set(target_row)
    arrived = lax.all_to_all(slot_rows, "seq", split_axis=0, concat_axis=0, tiled=True)
    picked = jnp.minimum(arrived, row_count - 1)
    where_from = (
        jnp.zeros((row_count,), jnp.int32)
        .at[arrived]
        .set(jnp.arange(buffer_rows, dtype=jnp.int32), mode="drop")
    )

    def place(pieces):
        return pieces[where_from]

    far_weights = fetch_far_weights(out_weight)
    send_qk = jnp.concatenate([send_q, send_k], 1)
    arrived_qk = lax.all_to_all(send_qk, "seq", split_axis=0, concat_axis=0, tiled=True)
    arrived_qk, far_weights = lax.optimization_barrier((arrived_qk, far_weights))
    received = (
        arrived_qk[:, :heads_here],
        arrived_qk[:, heads_here:],
        lax.all_to_all(send_v, "seq", split_axis=0, concat_axis=0, tiled=True),
    )
    result = attend_local(place(received[0]), place(received[1]), place(received[2]))
    outgoing = result[picked]
    split = heads_here // 2
    head_count = lax.axis_size("head")
    me = lax.axis_index("head")
    partner_w = weight_block(out_weight, me ^ 1)
    own_w = weight_block(out_weight, me)

    def dot(lhs, weight):
        return jnp.dot(
            lhs, weight, precision=lax.Precision.HIGH, preferred_element_type=jnp.float32
        )

    def exchange(lo, hi):
        back = lax.all_to_all(outgoing[:, lo:hi], "seq", split_axis=0, concat_axis=0, tiled=True)
        return back

    def half_terms(back, lo, hi):
        mixed = back[send_row].reshape(row_count, (hi - lo) * DH)
        far_mixed = lax.ppermute(mixed, "head", swap_pairs(head_count, 2))
        rows = slice(lo * DH, hi * DH)
        to_partner = dot(mixed, partner_w[rows]) + dot(far_mixed, far_weights[1, rows])
        to_own = dot(mixed, own_w[rows]) + dot(far_mixed, far_weights[0, rows])
        return to_partner, to_own

    first_partner, first_own = half_terms(exchange(0, split), 0, split)
    second_back = exchange(split, heads_here)
    second_back, first_partner, first_own = lax.optimization_barrier(
        (second_back, first_partner, first_own)
    )
    second_partner, second_own = half_terms(second_back, split, heads_here)
    for_partner = first_partner + second_partner
    from_partner = lax.ppermute(for_partner, "head", swap_pairs(head_count, 1))
    return first_own + second_own + from_partner


def swap_pairs(count, bit):
    return [(index, index ^ bit) for index in range(count)]


def weight_block(out_weight, index):
    width = out_weight.shape[1] // lax.axis_size("head")
    return lax.dynamic_slice_in_dim(out_weight, index * width, width, axis=1)


def fetch_far_weights(out_weight):
    head_count = lax.axis_size("head")
    me = lax.axis_index("head")
    outgoing = jnp.stack(
        [weight_block(out_weight, me ^ 2), weight_block(out_weight, me ^ 3)], 0
    )
    return lax.ppermute(outgoing, "head", swap_pairs(head_count, 2))


def solution(mesh):
    in_specs = (
        P("seq", "head"),
        P("seq", "head"),
        P("seq", "head"),
        P("seq"),
        P("seq"),
        P("seq"),
        P("head", None),
    )
    out_specs = P("seq", "head")
    return jax.shard_map(
        per_device, mesh=mesh, in_specs=in_specs, out_specs=out_specs, check_vma=False
    )
```

```python
import math

import jax
import jax.numpy as jnp
from jax import lax
from jax.sharding import PartitionSpec as P

DH = 128
CS = 1024
CL_DEV = 1


ROPE_BASE = 500000.0
ORIG_CONTEXT = 8192.0
STRETCH = 4.0
BETA_FAST = 32.0
BETA_SLOW = 1.0


def yarn_tables(token_pos, width):
    half_width = width // 2
    expo = jnp.arange(half_width, dtype=jnp.float32) * 2.0 / width
    theta = jnp.exp(-expo * math.log(ROPE_BASE))
    ratio = ORIG_CONTEXT * theta / (2.0 * math.pi)
    ramp = jnp.clip((ratio - BETA_SLOW) / (BETA_FAST - BETA_SLOW), 0.0, 1.0)
    freq = theta * (ramp + (1.0 - ramp) / STRETCH)
    angle = token_pos.astype(jnp.float32)[:, None] * freq[None, :]
    mscale = 0.1 * math.log(STRETCH) + 1.0
    cos_table = jnp.concatenate([jnp.cos(angle), jnp.cos(angle)], -1) * mscale
    sin_table = jnp.concatenate([jnp.sin(angle), jnp.sin(angle)], -1) * mscale
    return (cos_table[:, None, :], sin_table[:, None, :])


def rotate(field, cos_table, sin_table):
    half_width = field.shape[-1] // 2
    turned = jnp.concatenate([-field[..., half_width:], field[..., :half_width]], -1)
    return field * cos_table + turned * sin_table


def cluster_attention(triple):
    query_c, key_c, value_c = triple
    length = query_c.shape[0]
    scores = jnp.einsum(
        "qhd,khd->hqk", query_c, key_c, precision=lax.Precision.HIGH
    ) / math.sqrt(query_c.shape[-1])
    causal = jnp.arange(length)[:, None] >= jnp.arange(length)[None, :]
    scores = jnp.where(causal[None], scores, -jnp.inf)
    peak = jnp.max(scores, -1, keepdims=True)
    weights = jnp.exp(scores - peak)
    total = jnp.sum(weights, -1, keepdims=True)
    summed = jnp.einsum("hqk,khd->qhd", weights, value_c, precision=lax.Precision.HIGH)
    return summed / jnp.transpose(total, (1, 0, 2))


def attend_local(query_all, key_all, value_all):
    row_count, head_count, width = query_all.shape
    grouped = (
        query_all.reshape(row_count // CS, CS, head_count, width),
        key_all.reshape(row_count // CS, CS, head_count, width),
        value_all.reshape(row_count // CS, CS, head_count, width),
    )
    return lax.map(cluster_attention, grouped).reshape(row_count, head_count, width)


def per_device(queries, keys, values, positions, cluster, slot, out_weight):
    seq_count = lax.axis_size("seq")
    row_count = queries.shape[0]
    capacity = 3 * row_count // (2 * seq_count)
    buffer_rows = seq_count * capacity
    heads_here = queries.shape[1] // DH
    owner_ids = cluster // CL_DEV
    target_row = cluster % CL_DEV * CS + slot
    one_hot = (owner_ids[:, None] == jnp.arange(seq_count)[None, :]).astype(jnp.int32)
    token_rank = jnp.sum(jnp.cumsum(one_hot, 0) * one_hot, 1) - 1
    send_row = owner_ids * capacity + token_rank
    source_token = (
        jnp.full((buffer_rows,), row_count, jnp.int32)
        .at[send_row]
        .set(jnp.arange(row_count, dtype=jnp.int32))
    )
    shaped = (row_count, heads_here, DH)
    send_from = jnp.minimum(source_token, row_count - 1)
    send_q = queries.reshape(shaped)[send_from]
    send_k = keys.reshape(shaped)[send_from]
    send_v = values.reshape(shaped)[send_from]
    slot_rows = jnp.full((buffer_rows,), row_count, jnp.int32).at[send_row].set(target_row)
    index_rows = jnp.stack([slot_rows, positions[send_from]], 1)
    arrived_index = lax.all_to_all(index_rows, "seq", split_axis=0, concat_axis=0, tiled=True)
    arrived = arrived_index[:, 0]
    picked = jnp.minimum(arrived, row_count - 1)
    where_from = (
        jnp.zeros((row_count,), jnp.int32)
        .at[arrived]
        .set(jnp.arange(buffer_rows, dtype=jnp.int32), mode="drop")
    )

    def place(pieces):
        return pieces[where_from]

    far_weights = fetch_far_weights(out_weight)
    first_arrived = lax.all_to_all(send_q, "seq", split_axis=0, concat_axis=0, tiled=True)
    first_arrived, far_weights = lax.optimization_barrier((first_arrived, far_weights))
    received = (
        first_arrived,
        lax.all_to_all(send_k, "seq", split_axis=0, concat_axis=0, tiled=True),
        lax.all_to_all(send_v, "seq", split_axis=0, concat_axis=0, tiled=True),
    )
    cos_table, sin_table = yarn_tables(place(arrived_index[:, 1]), DH)
    result = attend_local(
        rotate(place(received[0]), cos_table, sin_table),
        rotate(place(received[1]), cos_table, sin_table),
        place(received[2]),
    )
    outgoing = result[picked]
    split = heads_here // 2
    head_count = lax.axis_size("head")
    me = lax.axis_index("head")
    partner_w = weight_block(out_weight, me ^ 1)
    own_w = weight_block(out_weight, me)

    def dot(lhs, weight):
        return jnp.dot(
            lhs, weight, precision=lax.Precision.HIGH, preferred_element_type=jnp.float32
        )

    def exchange(lo, hi):
        back = lax.all_to_all(outgoing[:, lo:hi], "seq", split_axis=0, concat_axis=0, tiled=True)
        return back

    def half_terms(back, lo, hi):
        mixed = back[send_row].reshape(row_count, (hi - lo) * DH)
        far_mixed = lax.ppermute(mixed, "head", swap_pairs(head_count, 2))
        rows = slice(lo * DH, hi * DH)
        to_partner = dot(mixed, partner_w[rows]) + dot(far_mixed, far_weights[1, rows])
        to_own = dot(mixed, own_w[rows]) + dot(far_mixed, far_weights[0, rows])
        return to_partner, to_own

    first_partner, first_own = half_terms(exchange(0, split), 0, split)
    second_back = exchange(split, heads_here)
    second_back, first_partner, first_own = lax.optimization_barrier(
        (second_back, first_partner, first_own)
    )
    second_partner, second_own = half_terms(second_back, split, heads_here)
    for_partner = first_partner + second_partner
    from_partner = lax.ppermute(for_partner, "head", swap_pairs(head_count, 1))
    return first_own + second_own + from_partner


def swap_pairs(count, bit):
    return [(index, index ^ bit) for index in range(count)]


def weight_block(out_weight, index):
    width = out_weight.shape[1] // lax.axis_size("head")
    return lax.dynamic_slice_in_dim(out_weight, index * width, width, axis=1)


def fetch_far_weights(out_weight):
    head_count = lax.axis_size("head")
    me = lax.axis_index("head")
    outgoing = jnp.stack(
        [weight_block(out_weight, me ^ 2), weight_block(out_weight, me ^ 3)], 0
    )
    return lax.ppermute(outgoing, "head", swap_pairs(head_count, 2))


def solution(mesh):
    in_specs = (
        P("seq", "head"),
        P("seq", "head"),
        P("seq", "head"),
        P("seq"),
        P("seq"),
        P("seq"),
        P("head", None),
    )
    out_specs = P("seq", "head")
    return jax.shard_map(
        per_device, mesh=mesh, in_specs=in_specs, out_specs=out_specs, check_vma=False
    )
```

```python
import math

import jax
import jax.numpy as jnp
from jax import lax
from jax.sharding import PartitionSpec as P

DH = 128
CS = 1024
CL_DEV = 1


ROPE_BASE = 500000.0
ORIG_CONTEXT = 8192.0
STRETCH = 4.0
BETA_FAST = 32.0
BETA_SLOW = 1.0


def yarn_tables(token_pos, width):
    half_width = width // 2
    expo = jnp.arange(half_width, dtype=jnp.float32) * 2.0 / width
    theta = jnp.exp(-expo * math.log(ROPE_BASE))
    ratio = ORIG_CONTEXT * theta / (2.0 * math.pi)
    ramp = jnp.clip((ratio - BETA_SLOW) / (BETA_FAST - BETA_SLOW), 0.0, 1.0)
    freq = theta * (ramp + (1.0 - ramp) / STRETCH)
    angle = token_pos.astype(jnp.float32)[:, None] * freq[None, :]
    mscale = 0.1 * math.log(STRETCH) + 1.0
    cos_table = jnp.concatenate([jnp.cos(angle), jnp.cos(angle)], -1) * mscale
    sin_table = jnp.concatenate([jnp.sin(angle), jnp.sin(angle)], -1) * mscale
    return (cos_table[:, None, :], sin_table[:, None, :])


def rotate(field, cos_table, sin_table):
    half_width = field.shape[-1] // 2
    turned = jnp.concatenate([-field[..., half_width:], field[..., :half_width]], -1)
    return field * cos_table + turned * sin_table


def cluster_attention(triple):
    query_c, key_c, value_c = triple
    length = query_c.shape[0]
    scores = jnp.einsum(
        "qhd,khd->hqk", query_c, key_c, precision=lax.Precision.HIGH
    ) / math.sqrt(query_c.shape[-1])
    causal = jnp.arange(length)[:, None] >= jnp.arange(length)[None, :]
    scores = jnp.where(causal[None], scores, -jnp.inf)
    peak = jnp.max(scores, -1, keepdims=True)
    weights = jnp.exp(scores - peak)
    total = jnp.sum(weights, -1, keepdims=True)
    summed = jnp.einsum("hqk,khd->qhd", weights, value_c, precision=lax.Precision.HIGH)
    return summed / jnp.transpose(total, (1, 0, 2))


def attend_local(query_all, key_all, value_all):
    row_count, head_count, width = query_all.shape
    grouped = (
        query_all.reshape(row_count // CS, CS, head_count, width),
        key_all.reshape(row_count // CS, CS, head_count, width),
        value_all.reshape(row_count // CS, CS, head_count, width),
    )
    return lax.map(cluster_attention, grouped).reshape(row_count, head_count, width)


def per_device(queries, keys, values, positions, cluster, slot, out_weight):
    seq_count = lax.axis_size("seq")
    row_count = queries.shape[0]
    capacity = 3 * row_count // (2 * seq_count)
    buffer_rows = seq_count * capacity
    heads_here = queries.shape[1] // DH
    owner_ids = cluster // CL_DEV
    target_row = cluster % CL_DEV * CS + slot
    one_hot = (owner_ids[:, None] == jnp.arange(seq_count)[None, :]).astype(jnp.int32)
    token_rank = jnp.sum(jnp.cumsum(one_hot, 0) * one_hot, 1) - 1
    send_row = owner_ids * capacity + token_rank
    source_token = (
        jnp.full((buffer_rows,), row_count, jnp.int32)
        .at[send_row]
        .set(jnp.arange(row_count, dtype=jnp.int32))
    )
    shaped = (row_count, heads_here, DH)
    send_from = jnp.minimum(source_token, row_count - 1)
    send_q = queries.reshape(shaped)[send_from]
    send_k = keys.reshape(shaped)[send_from]
    send_v = values.reshape(shaped)[send_from]
    index_rows = (
        jnp.full((buffer_rows, 2), row_count, jnp.int32)
        .at[send_row]
        .set(jnp.stack([target_row, positions], 1))
    )
    arrived_index = lax.all_to_all(index_rows, "seq", split_axis=0, concat_axis=0, tiled=True)
    arrived = arrived_index[:, 0]
    picked = jnp.minimum(arrived, row_count - 1)
    where_from = (
        jnp.zeros((row_count,), jnp.int32)
        .at[arrived]
        .set(jnp.arange(buffer_rows, dtype=jnp.int32), mode="drop")
    )

    def place(pieces):
        return pieces[where_from]

    far_weights = fetch_far_weights(out_weight)
    first_arrived = lax.all_to_all(send_q, "seq", split_axis=0, concat_axis=0, tiled=True)
    first_arrived, far_weights = lax.optimization_barrier((first_arrived, far_weights))
    received = (
        first_arrived,
        lax.all_to_all(send_k, "seq", split_axis=0, concat_axis=0, tiled=True),
        lax.all_to_all(send_v, "seq", split_axis=0, concat_axis=0, tiled=True),
    )
    cos_table, sin_table = yarn_tables(place(arrived_index[:, 1]), DH)
    result = attend_local(
        rotate(place(received[0]), cos_table, sin_table),
        rotate(place(received[1]), cos_table, sin_table),
        place(received[2]),
    )
    outgoing = result[picked]
    split = heads_here // 2
    head_count = lax.axis_size("head")
    me = lax.axis_index("head")
    partner_w = weight_block(out_weight, me ^ 1)
    own_w = weight_block(out_weight, me)

    def dot(lhs, weight):
        return jnp.dot(
            lhs, weight, precision=lax.Precision.HIGH, preferred_element_type=jnp.float32
        )

    def exchange(lo, hi):
        back = lax.all_to_all(outgoing[:, lo:hi], "seq", split_axis=0, concat_axis=0, tiled=True)
        return back

    def half_terms(back, lo, hi):
        mixed = back[send_row].reshape(row_count, (hi - lo) * DH)
        far_mixed = lax.ppermute(mixed, "head", swap_pairs(head_count, 2))
        rows = slice(lo * DH, hi * DH)
        to_partner = dot(mixed, partner_w[rows]) + dot(far_mixed, far_weights[1, rows])
        to_own = dot(mixed, own_w[rows]) + dot(far_mixed, far_weights[0, rows])
        return to_partner, to_own

    first_partner, first_own = half_terms(exchange(0, split), 0, split)
    second_back = exchange(split, heads_here)
    second_back, first_partner, first_own = lax.optimization_barrier(
        (second_back, first_partner, first_own)
    )
    second_partner, second_own = half_terms(second_back, split, heads_here)
    for_partner = first_partner + second_partner
    from_partner = lax.ppermute(for_partner, "head", swap_pairs(head_count, 1))
    return first_own + second_own + from_partner


def swap_pairs(count, bit):
    return [(index, index ^ bit) for index in range(count)]


def weight_block(out_weight, index):
    width = out_weight.shape[1] // lax.axis_size("head")
    return lax.dynamic_slice_in_dim(out_weight, index * width, width, axis=1)


def fetch_far_weights(out_weight):
    head_count = lax.axis_size("head")
    me = lax.axis_index("head")
    outgoing = jnp.stack(
        [weight_block(out_weight, me ^ 2), weight_block(out_weight, me ^ 3)], 0
    )
    return lax.ppermute(outgoing, "head", swap_pairs(head_count, 2))


def solution(mesh):
    in_specs = (
        P("seq", "head"),
        P("seq", "head"),
        P("seq", "head"),
        P("seq"),
        P("seq"),
        P("seq"),
        P("head", None),
    )
    out_specs = P("seq", "head")
    return jax.shard_map(
        per_device, mesh=mesh, in_specs=in_specs, out_specs=out_specs, check_vma=False
    )
```

```python
import math

import jax
import jax.numpy as jnp
from jax import lax
from jax.sharding import PartitionSpec as P

DH = 128
CS = 1024
CL_DEV = 1


ROPE_BASE = 500000.0
ORIG_CONTEXT = 8192.0
STRETCH = 4.0
BETA_FAST = 32.0
BETA_SLOW = 1.0


def yarn_tables(token_pos, width):
    half_width = width // 2
    expo = jnp.arange(half_width, dtype=jnp.float32) * 2.0 / width
    theta = jnp.exp(-expo * math.log(ROPE_BASE))
    ratio = ORIG_CONTEXT * theta / (2.0 * math.pi)
    ramp = jnp.clip((ratio - BETA_SLOW) / (BETA_FAST - BETA_SLOW), 0.0, 1.0)
    freq = theta * (ramp + (1.0 - ramp) / STRETCH)
    angle = token_pos.astype(jnp.float32)[:, None] * freq[None, :]
    mscale = 0.1 * math.log(STRETCH) + 1.0
    cos_table = jnp.concatenate([jnp.cos(angle), jnp.cos(angle)], -1) * mscale
    sin_table = jnp.concatenate([jnp.sin(angle), jnp.sin(angle)], -1) * mscale
    return (cos_table[:, None, :], sin_table[:, None, :])


def rotate(field, cos_table, sin_table):
    half_width = field.shape[-1] // 2
    turned = jnp.concatenate([-field[..., half_width:], field[..., :half_width]], -1)
    return field * cos_table + turned * sin_table


def cluster_attention(triple):
    query_c, key_c, value_c = triple
    length = query_c.shape[0]
    scores = jnp.einsum(
        "qhd,khd->hqk", query_c, key_c, precision=lax.Precision.HIGH
    ) / math.sqrt(query_c.shape[-1])
    causal = jnp.arange(length)[:, None] >= jnp.arange(length)[None, :]
    scores = jnp.where(causal[None], scores, -jnp.inf)
    peak = jnp.max(scores, -1, keepdims=True)
    weights = jnp.exp(scores - peak)
    total = jnp.sum(weights, -1, keepdims=True)
    summed = jnp.einsum("hqk,khd->qhd", weights, value_c, precision=lax.Precision.HIGH)
    return summed / jnp.transpose(total, (1, 0, 2))


def attend_local(query_all, key_all, value_all):
    row_count, head_count, width = query_all.shape
    grouped = (
        query_all.reshape(row_count // CS, CS, head_count, width),
        key_all.reshape(row_count // CS, CS, head_count, width),
        value_all.reshape(row_count // CS, CS, head_count, width),
    )
    return lax.map(cluster_attention, grouped).reshape(row_count, head_count, width)


def per_device(queries, keys, values, positions, cluster, slot, out_weight):
    seq_count = lax.axis_size("seq")
    row_count = queries.shape[0]
    capacity = 3 * row_count // (2 * seq_count)
    buffer_rows = seq_count * capacity
    heads_here = queries.shape[1] // DH
    owner_ids = cluster // CL_DEV
    target_row = cluster % CL_DEV * CS + slot
    one_hot = (owner_ids[:, None] == jnp.arange(seq_count)[None, :]).astype(jnp.int32)
    token_rank = jnp.sum(jnp.cumsum(one_hot, 0) * one_hot, 1) - 1
    send_row = owner_ids * capacity + token_rank
    source_token = (
        jnp.full((buffer_rows,), row_count, jnp.int32)
        .at[send_row]
        .set(jnp.arange(row_count, dtype=jnp.int32))
    )
    shaped = (row_count, heads_here, DH)
    send_from = jnp.minimum(source_token, row_count - 1)
    send_q = queries.reshape(shaped)[send_from]
    send_k = keys.reshape(shaped)[send_from]
    send_v = values.reshape(shaped)[send_from]
    index_rows = (
        jnp.full((buffer_rows, 2), row_count, jnp.int32)
        .at[send_row]
        .set(jnp.stack([target_row, positions], 1))
    )
    arrived_index = lax.all_to_all(index_rows, "seq", split_axis=0, concat_axis=0, tiled=True)
    arrived = arrived_index[:, 0]
    picked = jnp.minimum(arrived, row_count - 1)
    where_from = (
        jnp.zeros((row_count,), jnp.int32)
        .at[arrived]
        .set(jnp.arange(buffer_rows, dtype=jnp.int32), mode="drop")
    )

    def place(pieces):
        return pieces[where_from]

    far_weights = fetch_far_weights(out_weight)
    first_arrived = lax.all_to_all(send_q, "seq", split_axis=0, concat_axis=0, tiled=True)
    first_arrived, far_weights = lax.optimization_barrier((first_arrived, far_weights))
    received = (
        first_arrived,
        lax.all_to_all(send_k, "seq", split_axis=0, concat_axis=0, tiled=True),
        lax.all_to_all(send_v, "seq", split_axis=0, concat_axis=0, tiled=True),
    )
    cos_table, sin_table = yarn_tables(place(arrived_index[:, 1]), DH)
    result = attend_local(
        rotate(place(received[0]), cos_table, sin_table),
        rotate(place(received[1]), cos_table, sin_table),
        place(received[2]),
    )
    split = heads_here // 2
    head_count = lax.axis_size("head")
    me = lax.axis_index("head")
    partner_w = weight_block(out_weight, me ^ 1)
    own_w = weight_block(out_weight, me)

    def dot(lhs, weight):
        return jnp.dot(
            lhs, weight, precision=lax.Precision.HIGH, preferred_element_type=jnp.float32
        )

    def exchange(lo, hi):
        part = result[:, lo:hi][picked]
        back = lax.all_to_all(part, "seq", split_axis=0, concat_axis=0, tiled=True)
        return back

    def half_terms(back, lo, hi):
        mixed = back[send_row].reshape(row_count, (hi - lo) * DH)
        far_mixed = lax.ppermute(mixed, "head", swap_pairs(head_count, 2))
        rows = slice(lo * DH, hi * DH)
        to_partner = dot(mixed, partner_w[rows]) + dot(far_mixed, far_weights[1, rows])
        to_own = dot(mixed, own_w[rows]) + dot(far_mixed, far_weights[0, rows])
        return to_partner, to_own

    first_partner, first_own = half_terms(exchange(0, split), 0, split)
    second_back = exchange(split, heads_here)
    second_back, first_partner, first_own = lax.optimization_barrier(
        (second_back, first_partner, first_own)
    )
    second_partner, second_own = half_terms(second_back, split, heads_here)
    for_partner = first_partner + second_partner
    from_partner = lax.ppermute(for_partner, "head", swap_pairs(head_count, 1))
    return first_own + second_own + from_partner


def swap_pairs(count, bit):
    return [(index, index ^ bit) for index in range(count)]


def weight_block(out_weight, index):
    width = out_weight.shape[1] // lax.axis_size("head")
    return lax.dynamic_slice_in_dim(out_weight, index * width, width, axis=1)


def fetch_far_weights(out_weight):
    head_count = lax.axis_size("head")
    me = lax.axis_index("head")
    outgoing = jnp.stack(
        [weight_block(out_weight, me ^ 2), weight_block(out_weight, me ^ 3)], 0
    )
    return lax.ppermute(outgoing, "head", swap_pairs(head_count, 2))


def solution(mesh):
    in_specs = (
        P("seq", "head"),
        P("seq", "head"),
        P("seq", "head"),
        P("seq"),
        P("seq"),
        P("seq"),
        P("head", None),
    )
    out_specs = P("seq", "head")
    return jax.shard_map(
        per_device, mesh=mesh, in_specs=in_specs, out_specs=out_specs, check_vma=False
    )
```

```python
import math

import jax
import jax.numpy as jnp
from jax import lax
from jax.sharding import PartitionSpec as P

DH = 128
CS = 1024
CL_DEV = 1


ROPE_BASE = 500000.0
ORIG_CONTEXT = 8192.0
STRETCH = 4.0
BETA_FAST = 32.0
BETA_SLOW = 1.0


def yarn_tables(token_pos, width):
    half_width = width // 2
    expo = jnp.arange(half_width, dtype=jnp.float32) * 2.0 / width
    theta = jnp.exp(-expo * math.log(ROPE_BASE))
    ratio = ORIG_CONTEXT * theta / (2.0 * math.pi)
    ramp = jnp.clip((ratio - BETA_SLOW) / (BETA_FAST - BETA_SLOW), 0.0, 1.0)
    freq = theta * (ramp + (1.0 - ramp) / STRETCH)
    angle = token_pos.astype(jnp.float32)[:, None] * freq[None, :]
    mscale = 0.1 * math.log(STRETCH) + 1.0
    cos_table = jnp.concatenate([jnp.cos(angle), jnp.cos(angle)], -1) * mscale
    sin_table = jnp.concatenate([jnp.sin(angle), jnp.sin(angle)], -1) * mscale
    return (cos_table[:, None, :], sin_table[:, None, :])


def rotate(field, cos_table, sin_table):
    half_width = field.shape[-1] // 2
    turned = jnp.concatenate([-field[..., half_width:], field[..., :half_width]], -1)
    return field * cos_table + turned * sin_table


def cluster_attention(triple):
    query_c, key_c, value_c = triple
    length = query_c.shape[0]
    scores = jnp.einsum(
        "qhd,khd->hqk", query_c, key_c, precision=lax.Precision.HIGH
    ) / math.sqrt(query_c.shape[-1])
    causal = jnp.arange(length)[:, None] >= jnp.arange(length)[None, :]
    scores = jnp.where(causal[None], scores, -jnp.inf)
    peak = jnp.max(scores, -1, keepdims=True)
    weights = jnp.exp(scores - peak)
    total = jnp.sum(weights, -1, keepdims=True)
    split = query_c.shape[1] // 2
    parts = []
    for lo, hi in ((0, split), (split, query_c.shape[1])):
        summed = jnp.einsum(
            "hqk,khd->qhd", weights[lo:hi], value_c[:, lo:hi], precision=lax.Precision.HIGH
        )
        parts.append(summed / jnp.transpose(total[lo:hi], (1, 0, 2)))
    return tuple(parts)


def attend_local(query_all, key_all, value_all):
    row_count, head_count, width = query_all.shape
    grouped = (
        query_all.reshape(row_count // CS, CS, head_count, width),
        key_all.reshape(row_count // CS, CS, head_count, width),
        value_all.reshape(row_count // CS, CS, head_count, width),
    )
    parts = lax.map(cluster_attention, grouped)
    return [part.reshape(row_count, part.shape[2], width) for part in parts]


def per_device(queries, keys, values, positions, cluster, slot, out_weight):
    seq_count = lax.axis_size("seq")
    row_count = queries.shape[0]
    capacity = 3 * row_count // (2 * seq_count)
    buffer_rows = seq_count * capacity
    heads_here = queries.shape[1] // DH
    owner_ids = cluster // CL_DEV
    target_row = cluster % CL_DEV * CS + slot
    one_hot = (owner_ids[:, None] == jnp.arange(seq_count)[None, :]).astype(jnp.int32)
    token_rank = jnp.sum(jnp.cumsum(one_hot, 0) * one_hot, 1) - 1
    send_row = owner_ids * capacity + token_rank
    source_token = (
        jnp.full((buffer_rows,), row_count, jnp.int32)
        .at[send_row]
        .set(jnp.arange(row_count, dtype=jnp.int32))
    )
    shaped = (row_count, heads_here, DH)
    send_from = jnp.minimum(source_token, row_count - 1)
    send_q = queries.reshape(shaped)[send_from]
    send_k = keys.reshape(shaped)[send_from]
    send_v = values.reshape(shaped)[send_from]
    index_rows = (
        jnp.full((buffer_rows, 2), row_count, jnp.int32)
        .at[send_row]
        .set(jnp.stack([target_row, positions], 1))
    )
    arrived_index = lax.all_to_all(index_rows, "seq", split_axis=0, concat_axis=0, tiled=True)
    arrived = arrived_index[:, 0]
    picked = jnp.minimum(arrived, row_count - 1)
    where_from = (
        jnp.zeros((row_count,), jnp.int32)
        .at[arrived]
        .set(jnp.arange(buffer_rows, dtype=jnp.int32), mode="drop")
    )

    def place(pieces):
        return pieces[where_from]

    far_weights = fetch_far_weights(out_weight)
    first_arrived = lax.all_to_all(send_q, "seq", split_axis=0, concat_axis=0, tiled=True)
    first_arrived, far_weights = lax.optimization_barrier((first_arrived, far_weights))
    received = (
        first_arrived,
        lax.all_to_all(send_k, "seq", split_axis=0, concat_axis=0, tiled=True),
        lax.all_to_all(send_v, "seq", split_axis=0, concat_axis=0, tiled=True),
    )
    cos_table, sin_table = yarn_tables(place(arrived_index[:, 1]), DH)
    result = attend_local(
        rotate(place(received[0]), cos_table, sin_table),
        rotate(place(received[1]), cos_table, sin_table),
        place(received[2]),
    )
    split = heads_here // 2
    head_count = lax.axis_size("head")
    me = lax.axis_index("head")
    partner_w = weight_block(out_weight, me ^ 1)
    own_w = weight_block(out_weight, me)

    def dot(lhs, weight):
        return jnp.dot(
            lhs, weight, precision=lax.Precision.HIGH, preferred_element_type=jnp.float32
        )

    def exchange(lo, hi):
        part = result[0 if lo == 0 else 1][picked]
        back = lax.all_to_all(part, "seq", split_axis=0, concat_axis=0, tiled=True)
        return back

    def half_terms(back, lo, hi):
        mixed = back[send_row].reshape(row_count, (hi - lo) * DH)
        far_mixed = lax.ppermute(mixed, "head", swap_pairs(head_count, 2))
        rows = slice(lo * DH, hi * DH)
        to_partner = dot(mixed, partner_w[rows]) + dot(far_mixed, far_weights[1, rows])
        to_own = dot(mixed, own_w[rows]) + dot(far_mixed, far_weights[0, rows])
        return to_partner, to_own

    first_partner, first_own = half_terms(exchange(0, split), 0, split)
    second_back = exchange(split, heads_here)
    second_back, first_partner, first_own = lax.optimization_barrier(
        (second_back, first_partner, first_own)
    )
    second_partner, second_own = half_terms(second_back, split, heads_here)
    for_partner = first_partner + second_partner
    from_partner = lax.ppermute(for_partner, "head", swap_pairs(head_count, 1))
    return first_own + second_own + from_partner


def swap_pairs(count, bit):
    return [(index, index ^ bit) for index in range(count)]


def weight_block(out_weight, index):
    width = out_weight.shape[1] // lax.axis_size("head")
    return lax.dynamic_slice_in_dim(out_weight, index * width, width, axis=1)


def fetch_far_weights(out_weight):
    head_count = lax.axis_size("head")
    me = lax.axis_index("head")
    outgoing = jnp.stack(
        [weight_block(out_weight, me ^ 2), weight_block(out_weight, me ^ 3)], 0
    )
    return lax.ppermute(outgoing, "head", swap_pairs(head_count, 2))


def solution(mesh):
    in_specs = (
        P("seq", "head"),
        P("seq", "head"),
        P("seq", "head"),
        P("seq"),
        P("seq"),
        P("seq"),
        P("head", None),
    )
    out_specs = P("seq", "head")
    return jax.shard_map(
        per_device, mesh=mesh, in_specs=in_specs, out_specs=out_specs, check_vma=False
    )
```

```python
import math

import jax
import jax.numpy as jnp
from jax import lax
from jax.sharding import PartitionSpec as P

DH = 128
CS = 1024
CL_DEV = 1


ROPE_BASE = 500000.0
ORIG_CONTEXT = 8192.0
STRETCH = 4.0
BETA_FAST = 32.0
BETA_SLOW = 1.0


def yarn_tables(token_pos, width):
    half_width = width // 2
    expo = jnp.arange(half_width, dtype=jnp.float32) * 2.0 / width
    theta = jnp.exp(-expo * math.log(ROPE_BASE))
    ratio = ORIG_CONTEXT * theta / (2.0 * math.pi)
    ramp = jnp.clip((ratio - BETA_SLOW) / (BETA_FAST - BETA_SLOW), 0.0, 1.0)
    freq = theta * (ramp + (1.0 - ramp) / STRETCH)
    angle = token_pos.astype(jnp.float32)[:, None] * freq[None, :]
    mscale = 0.1 * math.log(STRETCH) + 1.0
    cos_table = jnp.concatenate([jnp.cos(angle), jnp.cos(angle)], -1) * mscale
    sin_table = jnp.concatenate([jnp.sin(angle), jnp.sin(angle)], -1) * mscale
    return (cos_table[:, None, :], sin_table[:, None, :])


def rotate(field, cos_table, sin_table):
    half_width = field.shape[-1] // 2
    turned = jnp.concatenate([-field[..., half_width:], field[..., :half_width]], -1)
    return field * cos_table + turned * sin_table


def cluster_attention(triple):
    query_c, key_c, value_c = triple
    length = query_c.shape[0]
    scores = jnp.einsum(
        "qhd,khd->hqk", query_c, key_c, precision=lax.Precision.HIGH
    ) / math.sqrt(query_c.shape[-1])
    causal = jnp.arange(length)[:, None] >= jnp.arange(length)[None, :]
    scores = jnp.where(causal[None], scores, -jnp.inf)
    peak = jnp.max(scores, -1, keepdims=True)
    weights = jnp.exp(scores - peak)
    total = jnp.sum(weights, -1, keepdims=True)
    split = query_c.shape[1] // 2
    parts = []
    for lo, hi in ((0, split), (split, query_c.shape[1])):
        summed = jnp.einsum(
            "hqk,khd->qhd", weights[lo:hi], value_c[:, lo:hi], precision=lax.Precision.HIGH
        )
        parts.append(summed / jnp.transpose(total[lo:hi], (1, 0, 2)))
    return tuple(parts)


def attend_local(query_all, key_all, value_all):
    row_count, head_count, width = query_all.shape
    grouped = (
        query_all.reshape(row_count // CS, CS, head_count, width),
        key_all.reshape(row_count // CS, CS, head_count, width),
        value_all.reshape(row_count // CS, CS, head_count, width),
    )
    parts = lax.map(cluster_attention, grouped)
    return [part.reshape(row_count, part.shape[2], width) for part in parts]


def per_device(queries, keys, values, positions, cluster, slot, out_weight):
    seq_count = lax.axis_size("seq")
    row_count = queries.shape[0]
    capacity = 3 * row_count // (2 * seq_count)
    buffer_rows = seq_count * capacity
    heads_here = queries.shape[1] // DH
    owner_ids = cluster // CL_DEV
    target_row = cluster % CL_DEV * CS + slot
    one_hot = (owner_ids[:, None] == jnp.arange(seq_count)[None, :]).astype(jnp.int32)
    token_rank = jnp.sum(jnp.cumsum(one_hot, 0) * one_hot, 1) - 1
    send_row = owner_ids * capacity + token_rank
    source_token = (
        jnp.full((buffer_rows,), row_count, jnp.int32)
        .at[send_row]
        .set(jnp.arange(row_count, dtype=jnp.int32))
    )
    shaped = (row_count, heads_here, DH)
    send_from = jnp.minimum(source_token, row_count - 1)
    send_q = queries.reshape(shaped)[send_from]
    send_k = keys.reshape(shaped)[send_from]
    send_v = values.reshape(shaped)[send_from]
    index_rows = (
        jnp.full((buffer_rows, 2), row_count, jnp.int32)
        .at[send_row]
        .set(jnp.stack([target_row, positions], 1))
    )
    arrived_index = lax.all_to_all(index_rows, "seq", split_axis=0, concat_axis=0, tiled=True)
    arrived = arrived_index[:, 0]
    picked = jnp.minimum(arrived, row_count - 1)
    where_from = (
        jnp.zeros((row_count,), jnp.int32)
        .at[arrived]
        .set(jnp.arange(buffer_rows, dtype=jnp.int32), mode="drop")
    )

    def place(pieces):
        return pieces[where_from]

    far_weights = fetch_far_weights(out_weight)
    first_arrived = lax.all_to_all(send_q, "seq", split_axis=0, concat_axis=0, tiled=True)
    first_arrived, far_weights = lax.optimization_barrier((first_arrived, far_weights))
    received = (
        first_arrived,
        lax.all_to_all(send_k, "seq", split_axis=0, concat_axis=0, tiled=True),
        lax.all_to_all(send_v, "seq", split_axis=0, concat_axis=0, tiled=True),
    )
    cos_table, sin_table = yarn_tables(place(arrived_index[:, 1]), DH)
    result = attend_local(
        rotate(place(received[0]), cos_table, sin_table),
        rotate(place(received[1]), cos_table, sin_table),
        place(received[2]),
    )
    split = heads_here // 2
    head_count = lax.axis_size("head")
    me = lax.axis_index("head")
    partner_w = weight_block(out_weight, me ^ 1)
    own_w = weight_block(out_weight, me)

    def dot(lhs, weight):
        return jnp.dot(
            lhs, weight, precision=lax.Precision.HIGH, preferred_element_type=jnp.float32
        )

    def exchange(lo, hi):
        part = result[0 if lo == 0 else 1][picked]
        back = lax.all_to_all(part, "seq", split_axis=0, concat_axis=0, tiled=True)
        return back

    def half_terms(back, lo, hi, start_partner, start_own):
        mixed = back[send_row].reshape(row_count, (hi - lo) * DH)
        far_mixed = lax.ppermute(mixed, "head", swap_pairs(head_count, 2))
        rows = slice(lo * DH, hi * DH)
        near_partner = start_partner + dot(mixed, partner_w[rows])
        near_own = start_own + dot(mixed, own_w[rows])
        far_mixed, near_partner, near_own = lax.optimization_barrier(
            (far_mixed, near_partner, near_own)
        )
        to_partner = near_partner + dot(far_mixed, far_weights[1, rows])
        to_own = near_own + dot(far_mixed, far_weights[0, rows])
        return to_partner, to_own

    zero = jnp.zeros((row_count, partner_w.shape[1]), jnp.float32)
    first_partner, first_own = half_terms(exchange(0, split), 0, split, zero, zero)
    second_back = exchange(split, heads_here)
    second_back, first_partner, first_own = lax.optimization_barrier(
        (second_back, first_partner, first_own)
    )
    for_partner, own = half_terms(second_back, split, heads_here, first_partner, first_own)
    from_partner = lax.ppermute(for_partner, "head", swap_pairs(head_count, 1))
    return own + from_partner


def swap_pairs(count, bit):
    return [(index, index ^ bit) for index in range(count)]


def weight_block(out_weight, index):
    width = out_weight.shape[1] // lax.axis_size("head")
    return lax.dynamic_slice_in_dim(out_weight, index * width, width, axis=1)


def fetch_far_weights(out_weight):
    head_count = lax.axis_size("head")
    me = lax.axis_index("head")
    outgoing = jnp.stack(
        [weight_block(out_weight, me ^ 2), weight_block(out_weight, me ^ 3)], 0
    )
    return lax.ppermute(outgoing, "head", swap_pairs(head_count, 2))


def solution(mesh):
    in_specs = (
        P("seq", "head"),
        P("seq", "head"),
        P("seq", "head"),
        P("seq"),
        P("seq"),
        P("seq"),
        P("head", None),
    )
    out_specs = P("seq", "head")
    return jax.shard_map(
        per_device, mesh=mesh, in_specs=in_specs, out_specs=out_specs, check_vma=False
    )
```

```python
import math

import jax
import jax.numpy as jnp
from jax import lax
from jax.sharding import PartitionSpec as P

DH = 128
CS = 1024
CL_DEV = 1


ROPE_BASE = 500000.0
ORIG_CONTEXT = 8192.0
STRETCH = 4.0
BETA_FAST = 32.0
BETA_SLOW = 1.0


def yarn_tables(token_pos, width):
    half_width = width // 2
    expo = jnp.arange(half_width, dtype=jnp.float32) * 2.0 / width
    theta = jnp.exp(-expo * math.log(ROPE_BASE))
    ratio = ORIG_CONTEXT * theta / (2.0 * math.pi)
    ramp = jnp.clip((ratio - BETA_SLOW) / (BETA_FAST - BETA_SLOW), 0.0, 1.0)
    freq = theta * (ramp + (1.0 - ramp) / STRETCH)
    angle = token_pos.astype(jnp.float32)[:, None] * freq[None, :]
    mscale = 0.1 * math.log(STRETCH) + 1.0
    cos_table = jnp.concatenate([jnp.cos(angle), jnp.cos(angle)], -1) * mscale
    sin_table = jnp.concatenate([jnp.sin(angle), jnp.sin(angle)], -1) * mscale
    return (cos_table[:, None, :], sin_table[:, None, :])


def rotate(field, cos_table, sin_table):
    half_width = field.shape[-1] // 2
    turned = jnp.concatenate([-field[..., half_width:], field[..., :half_width]], -1)
    return field * cos_table + turned * sin_table


def cluster_attention(triple):
    query_c, key_c, value_c = triple
    length = query_c.shape[0]
    scores = jnp.einsum(
        "qhd,khd->hqk", query_c, key_c, precision=lax.Precision.HIGH
    ) / math.sqrt(query_c.shape[-1])
    causal = jnp.arange(length)[:, None] >= jnp.arange(length)[None, :]
    scores = jnp.where(causal[None], scores, -jnp.inf)
    peak = jnp.max(scores, -1, keepdims=True)
    weights = jnp.exp(scores - peak)
    total = jnp.sum(weights, -1, keepdims=True)
    split = query_c.shape[1] // 2
    parts = []
    for lo, hi in ((0, split), (split, query_c.shape[1])):
        summed = jnp.einsum(
            "hqk,khd->qhd", weights[lo:hi], value_c[:, lo:hi], precision=lax.Precision.HIGH
        )
        parts.append(summed / jnp.transpose(total[lo:hi], (1, 0, 2)))
    return tuple(parts)


def attend_local(query_all, key_all, value_all):
    row_count, head_count, width = query_all.shape
    grouped = (
        query_all.reshape(row_count // CS, CS, head_count, width),
        key_all.reshape(row_count // CS, CS, head_count, width),
        value_all.reshape(row_count // CS, CS, head_count, width),
    )
    parts = lax.map(cluster_attention, grouped)
    return [part.reshape(row_count, part.shape[2], width) for part in parts]


def per_device(queries, keys, values, positions, cluster, slot, out_weight):
    seq_count = lax.axis_size("seq")
    row_count = queries.shape[0]
    capacity = 3 * row_count // (2 * seq_count)
    buffer_rows = seq_count * capacity
    heads_here = queries.shape[1] // DH
    owner_ids = cluster // CL_DEV
    target_row = cluster % CL_DEV * CS + slot
    one_hot = (owner_ids[:, None] == jnp.arange(seq_count)[None, :]).astype(jnp.int32)
    token_rank = jnp.sum(jnp.cumsum(one_hot, 0) * one_hot, 1) - 1
    send_row = owner_ids * capacity + token_rank
    source_token = (
        jnp.full((buffer_rows,), row_count, jnp.int32)
        .at[send_row]
        .set(jnp.arange(row_count, dtype=jnp.int32))
    )
    shaped = (row_count, heads_here, DH)
    send_from = jnp.minimum(source_token, row_count - 1)
    send_q = queries.reshape(shaped)[send_from]
    send_k = keys.reshape(shaped)[send_from]
    send_v = values.reshape(shaped)[send_from]
    index_rows = (
        jnp.full((buffer_rows, 2), row_count, jnp.int32)
        .at[send_row]
        .set(jnp.stack([target_row, positions], 1))
    )
    arrived_index = lax.all_to_all(index_rows, "seq", split_axis=0, concat_axis=0, tiled=True)
    arrived = arrived_index[:, 0]
    picked = jnp.minimum(arrived, row_count - 1)
    where_from = (
        jnp.zeros((row_count,), jnp.int32)
        .at[arrived]
        .set(jnp.arange(buffer_rows, dtype=jnp.int32), mode="drop")
    )

    def place(pieces):
        return pieces[where_from]

    far_weights = fetch_far_weights(out_weight)
    first_arrived = lax.all_to_all(send_q, "seq", split_axis=0, concat_axis=0, tiled=True)
    first_arrived, far_weights = lax.optimization_barrier((first_arrived, far_weights))
    received = (
        first_arrived,
        lax.all_to_all(send_k, "seq", split_axis=0, concat_axis=0, tiled=True),
        lax.all_to_all(send_v, "seq", split_axis=0, concat_axis=0, tiled=True),
    )
    cos_table, sin_table = yarn_tables(place(arrived_index[:, 1]), DH)
    result = attend_local(
        rotate(place(received[0]), cos_table, sin_table),
        rotate(place(received[1]), cos_table, sin_table),
        place(received[2]),
    )
    split = heads_here // 2
    head_count = lax.axis_size("head")
    me = lax.axis_index("head")
    partner_w = weight_block(out_weight, me ^ 1)
    own_w = weight_block(out_weight, me)

    def dot(lhs, weight):
        return jnp.dot(
            lhs, weight, precision=lax.Precision.HIGH, preferred_element_type=jnp.float32
        )

    def exchange(lo, hi):
        part = result[0 if lo == 0 else 1][picked]
        back = lax.all_to_all(part, "seq", split_axis=0, concat_axis=0, tiled=True)
        return back

    def half_terms(back, lo, hi, start_partner, start_own, hold):
        mixed = back[send_row].reshape(row_count, (hi - lo) * DH)
        far_mixed = lax.ppermute(mixed, "head", swap_pairs(head_count, 2))
        rows = slice(lo * DH, hi * DH)
        near_partner = dot(mixed, partner_w[rows])
        near_own = dot(mixed, own_w[rows])
        if start_partner is not None:
            near_partner = start_partner + near_partner
            near_own = start_own + near_own
        if hold:
            far_mixed, near_partner, near_own = lax.optimization_barrier(
                (far_mixed, near_partner, near_own)
            )
        to_partner = near_partner + dot(far_mixed, far_weights[1, rows])
        to_own = near_own + dot(far_mixed, far_weights[0, rows])
        return to_partner, to_own

    first_partner, first_own = half_terms(exchange(0, split), 0, split, None, None, False)
    second_back = exchange(split, heads_here)
    second_back, first_partner, first_own = lax.optimization_barrier(
        (second_back, first_partner, first_own)
    )
    for_partner, own = half_terms(
        second_back, split, heads_here, first_partner, first_own, True
    )
    from_partner = lax.ppermute(for_partner, "head", swap_pairs(head_count, 1))
    return own + from_partner


def swap_pairs(count, bit):
    return [(index, index ^ bit) for index in range(count)]


def weight_block(out_weight, index):
    width = out_weight.shape[1] // lax.axis_size("head")
    return lax.dynamic_slice_in_dim(out_weight, index * width, width, axis=1)


def fetch_far_weights(out_weight):
    head_count = lax.axis_size("head")
    me = lax.axis_index("head")
    outgoing = jnp.stack(
        [weight_block(out_weight, me ^ 2), weight_block(out_weight, me ^ 3)], 0
    )
    return lax.ppermute(outgoing, "head", swap_pairs(head_count, 2))


def solution(mesh):
    in_specs = (
        P("seq", "head"),
        P("seq", "head"),
        P("seq", "head"),
        P("seq"),
        P("seq"),
        P("seq"),
        P("head", None),
    )
    out_specs = P("seq", "head")
    return jax.shard_map(
        per_device, mesh=mesh, in_specs=in_specs, out_specs=out_specs, check_vma=False
    )
```

```python
import math

import jax
import jax.numpy as jnp
from jax import lax
from jax.sharding import PartitionSpec as P

DH = 128
CS = 1024
CL_DEV = 1


ROPE_BASE = 500000.0
ORIG_CONTEXT = 8192.0
STRETCH = 4.0
BETA_FAST = 32.0
BETA_SLOW = 1.0


def yarn_tables(token_pos, width):
    half_width = width // 2
    expo = jnp.arange(half_width, dtype=jnp.float32) * 2.0 / width
    theta = jnp.exp(-expo * math.log(ROPE_BASE))
    ratio = ORIG_CONTEXT * theta / (2.0 * math.pi)
    ramp = jnp.clip((ratio - BETA_SLOW) / (BETA_FAST - BETA_SLOW), 0.0, 1.0)
    freq = theta * (ramp + (1.0 - ramp) / STRETCH)
    angle = token_pos.astype(jnp.float32)[:, None] * freq[None, :]
    mscale = 0.1 * math.log(STRETCH) + 1.0
    cos_table = jnp.concatenate([jnp.cos(angle), jnp.cos(angle)], -1) * mscale
    sin_table = jnp.concatenate([jnp.sin(angle), jnp.sin(angle)], -1) * mscale
    return (cos_table[:, None, :], sin_table[:, None, :])


def rotate(field, cos_table, sin_table):
    half_width = field.shape[-1] // 2
    turned = jnp.concatenate([-field[..., half_width:], field[..., :half_width]], -1)
    return field * cos_table + turned * sin_table


def cluster_attention(triple):
    query_c, key_c, value_c = triple
    length = query_c.shape[0]
    scores = jnp.einsum(
        "qhd,khd->hqk", query_c, key_c, precision=lax.Precision.HIGH
    ) / math.sqrt(query_c.shape[-1])
    causal = jnp.arange(length)[:, None] >= jnp.arange(length)[None, :]
    scores = jnp.where(causal[None], scores, -jnp.inf)
    peak = jnp.max(scores, -1, keepdims=True)
    weights = jnp.exp(scores - peak)
    total = jnp.sum(weights, -1, keepdims=True)
    split = query_c.shape[1] // 2
    parts = []
    for (lo, hi), value_part in zip(((0, split), (split, query_c.shape[1])), value_c):
        summed = jnp.einsum(
            "hqk,khd->qhd", weights[lo:hi], value_part, precision=lax.Precision.HIGH
        )
        parts.append(summed / jnp.transpose(total[lo:hi], (1, 0, 2)))
    return tuple(parts)


def attend_local(query_all, key_all, value_all):
    row_count, head_count, width = query_all.shape
    grouped = (
        query_all.reshape(row_count // CS, CS, head_count, width),
        key_all.reshape(row_count // CS, CS, head_count, width),
        tuple(
            part.reshape(row_count // CS, CS, part.shape[1], width) for part in value_all
        ),
    )
    parts = lax.map(cluster_attention, grouped)
    return [part.reshape(row_count, part.shape[2], width) for part in parts]


def per_device(queries, keys, values, positions, cluster, slot, out_weight):
    seq_count = lax.axis_size("seq")
    row_count = queries.shape[0]
    capacity = 3 * row_count // (2 * seq_count)
    buffer_rows = seq_count * capacity
    heads_here = queries.shape[1] // DH
    owner_ids = cluster // CL_DEV
    target_row = cluster % CL_DEV * CS + slot
    one_hot = (owner_ids[:, None] == jnp.arange(seq_count)[None, :]).astype(jnp.int32)
    token_rank = jnp.sum(jnp.cumsum(one_hot, 0) * one_hot, 1) - 1
    send_row = owner_ids * capacity + token_rank
    source_token = (
        jnp.full((buffer_rows,), row_count, jnp.int32)
        .at[send_row]
        .set(jnp.arange(row_count, dtype=jnp.int32))
    )
    shaped = (row_count, heads_here, DH)
    send_from = jnp.minimum(source_token, row_count - 1)
    send_q = queries.reshape(shaped)[send_from]
    send_k = keys.reshape(shaped)[send_from]
    send_v = values.reshape(shaped)[send_from]
    index_rows = (
        jnp.full((buffer_rows, 2), row_count, jnp.int32)
        .at[send_row]
        .set(jnp.stack([target_row, positions], 1))
    )
    arrived_index = lax.all_to_all(index_rows, "seq", split_axis=0, concat_axis=0, tiled=True)
    arrived = arrived_index[:, 0]
    picked = jnp.minimum(arrived, row_count - 1)
    where_from = (
        jnp.zeros((row_count,), jnp.int32)
        .at[arrived]
        .set(jnp.arange(buffer_rows, dtype=jnp.int32), mode="drop")
    )

    def place(pieces):
        return pieces[where_from]

    far_weights = fetch_far_weights(out_weight)
    first_arrived = lax.all_to_all(send_q, "seq", split_axis=0, concat_axis=0, tiled=True)
    first_arrived, far_weights = lax.optimization_barrier((first_arrived, far_weights))
    received = (
        first_arrived,
        lax.all_to_all(send_k, "seq", split_axis=0, concat_axis=0, tiled=True),
        tuple(
            lax.all_to_all(send_v[:, lo:hi], "seq", split_axis=0, concat_axis=0, tiled=True)
            for lo, hi in ((0, heads_here // 2), (heads_here // 2, heads_here))
        ),
    )
    cos_table, sin_table = yarn_tables(place(arrived_index[:, 1]), DH)
    result = attend_local(
        rotate(place(received[0]), cos_table, sin_table),
        rotate(place(received[1]), cos_table, sin_table),
        tuple(place(part) for part in received[2]),
    )
    split = heads_here // 2
    head_count = lax.axis_size("head")
    me = lax.axis_index("head")
    partner_w = weight_block(out_weight, me ^ 1)
    own_w = weight_block(out_weight, me)

    def dot(lhs, weight):
        return jnp.dot(
            lhs, weight, precision=lax.Precision.HIGH, preferred_element_type=jnp.float32
        )

    def exchange(lo, hi):
        part = result[0 if lo == 0 else 1][picked]
        back = lax.all_to_all(part, "seq", split_axis=0, concat_axis=0, tiled=True)
        return back

    def half_terms(back, lo, hi, start_partner, start_own, hold):
        mixed = back[send_row].reshape(row_count, (hi - lo) * DH)
        far_mixed = lax.ppermute(mixed, "head", swap_pairs(head_count, 2))
        rows = slice(lo * DH, hi * DH)
        near_partner = dot(mixed, partner_w[rows])
        near_own = dot(mixed, own_w[rows])
        if start_partner is not None:
            near_partner = start_partner + near_partner
            near_own = start_own + near_own
        if hold:
            far_mixed, near_partner, near_own = lax.optimization_barrier(
                (far_mixed, near_partner, near_own)
            )
        to_partner = near_partner + dot(far_mixed, far_weights[1, rows])
        to_own = near_own + dot(far_mixed, far_weights[0, rows])
        return to_partner, to_own

    first_partner, first_own = half_terms(exchange(0, split), 0, split, None, None, False)
    second_back = exchange(split, heads_here)
    second_back, first_partner, first_own = lax.optimization_barrier(
        (second_back, first_partner, first_own)
    )
    for_partner, own = half_terms(
        second_back, split, heads_here, first_partner, first_own, True
    )
    from_partner = lax.ppermute(for_partner, "head", swap_pairs(head_count, 1))
    return own + from_partner


def swap_pairs(count, bit):
    return [(index, index ^ bit) for index in range(count)]


def weight_block(out_weight, index):
    width = out_weight.shape[1] // lax.axis_size("head")
    return lax.dynamic_slice_in_dim(out_weight, index * width, width, axis=1)


def fetch_far_weights(out_weight):
    head_count = lax.axis_size("head")
    me = lax.axis_index("head")
    outgoing = jnp.stack(
        [weight_block(out_weight, me ^ 2), weight_block(out_weight, me ^ 3)], 0
    )
    return lax.ppermute(outgoing, "head", swap_pairs(head_count, 2))


def solution(mesh):
    in_specs = (
        P("seq", "head"),
        P("seq", "head"),
        P("seq", "head"),
        P("seq"),
        P("seq"),
        P("seq"),
        P("head", None),
    )
    out_specs = P("seq", "head")
    return jax.shard_map(
        per_device, mesh=mesh, in_specs=in_specs, out_specs=out_specs, check_vma=False
    )
```

```python
import math

import jax
import jax.numpy as jnp
from jax import lax
from jax.sharding import PartitionSpec as P

DH = 128
CS = 1024
CL_DEV = 1


ROPE_BASE = 500000.0
ORIG_CONTEXT = 8192.0
STRETCH = 4.0
BETA_FAST = 32.0
BETA_SLOW = 1.0


def yarn_tables(token_pos, width):
    half_width = width // 2
    expo = jnp.arange(half_width, dtype=jnp.float32) * 2.0 / width
    theta = jnp.exp(-expo * math.log(ROPE_BASE))
    ratio = ORIG_CONTEXT * theta / (2.0 * math.pi)
    ramp = jnp.clip((ratio - BETA_SLOW) / (BETA_FAST - BETA_SLOW), 0.0, 1.0)
    freq = theta * (ramp + (1.0 - ramp) / STRETCH)
    angle = token_pos.astype(jnp.float32)[:, None] * freq[None, :]
    mscale = 0.1 * math.log(STRETCH) + 1.0
    cos_table = jnp.concatenate([jnp.cos(angle), jnp.cos(angle)], -1) * mscale
    sin_table = jnp.concatenate([jnp.sin(angle), jnp.sin(angle)], -1) * mscale
    return (cos_table[:, None, :], sin_table[:, None, :])


def rotate(field, cos_table, sin_table):
    half_width = field.shape[-1] // 2
    turned = jnp.concatenate([-field[..., half_width:], field[..., :half_width]], -1)
    return field * cos_table + turned * sin_table


def cluster_attention(triple):
    query_c, key_c, value_c = triple
    length = query_c.shape[0]
    scores = jnp.einsum(
        "qhd,khd->hqk", query_c, key_c, precision=lax.Precision.HIGH
    ) / math.sqrt(query_c.shape[-1])
    causal = jnp.arange(length)[:, None] >= jnp.arange(length)[None, :]
    scores = jnp.where(causal[None], scores, -jnp.inf)
    peak = jnp.max(scores, -1, keepdims=True)
    weights = jnp.exp(scores - peak)
    total = jnp.sum(weights, -1, keepdims=True)
    split = query_c.shape[1] // 2
    parts = []
    for lo, hi in ((0, split), (split, query_c.shape[1])):
        summed = jnp.einsum(
            "hqk,khd->qhd", weights[lo:hi], value_c[:, lo:hi], precision=lax.Precision.HIGH
        )
        parts.append(summed / jnp.transpose(total[lo:hi], (1, 0, 2)))
    return tuple(parts)


def attend_local(query_all, key_all, value_all):
    row_count, head_count, width = query_all.shape
    grouped = (
        query_all.reshape(row_count // CS, CS, head_count, width),
        key_all.reshape(row_count // CS, CS, head_count, width),
        value_all.reshape(row_count // CS, CS, head_count, width),
    )
    parts = lax.map(cluster_attention, grouped)
    return [part.reshape(row_count, part.shape[2], width) for part in parts]


def per_device(queries, keys, values, positions, cluster, slot, out_weight):
    seq_count = lax.axis_size("seq")
    row_count = queries.shape[0]
    capacity = 3 * row_count // (2 * seq_count)
    buffer_rows = seq_count * capacity
    heads_here = queries.shape[1] // DH
    owner_ids = cluster // CL_DEV
    target_row = cluster % CL_DEV * CS + slot
    one_hot = (owner_ids[:, None] == jnp.arange(seq_count)[None, :]).astype(jnp.int32)
    token_rank = jnp.sum(jnp.cumsum(one_hot, 0) * one_hot, 1) - 1
    send_row = owner_ids * capacity + token_rank
    source_token = (
        jnp.full((buffer_rows,), row_count, jnp.int32)
        .at[send_row]
        .set(jnp.arange(row_count, dtype=jnp.int32))
    )
    shaped = (row_count, heads_here, DH)
    send_from = jnp.minimum(source_token, row_count - 1)
    send_q = queries[send_from]
    send_k = keys[send_from]
    send_v = values.reshape(shaped)[send_from]
    index_rows = (
        jnp.full((buffer_rows, 2), row_count, jnp.int32)
        .at[send_row]
        .set(jnp.stack([target_row, positions], 1))
    )
    arrived_index = lax.all_to_all(index_rows, "seq", split_axis=0, concat_axis=0, tiled=True)
    arrived = arrived_index[:, 0]
    picked = jnp.minimum(arrived, row_count - 1)
    where_from = (
        jnp.zeros((row_count,), jnp.int32)
        .at[arrived]
        .set(jnp.arange(buffer_rows, dtype=jnp.int32), mode="drop")
    )

    def place(pieces):
        return pieces[where_from]

    far_weights = fetch_far_weights(out_weight)
    first_arrived = lax.all_to_all(send_q, "seq", split_axis=0, concat_axis=0, tiled=True)
    first_arrived, far_weights = lax.optimization_barrier((first_arrived, far_weights))
    received = (
        first_arrived,
        lax.all_to_all(send_k, "seq", split_axis=0, concat_axis=0, tiled=True),
        lax.all_to_all(send_v, "seq", split_axis=0, concat_axis=0, tiled=True),
    )
    cos_table, sin_table = yarn_tables(place(arrived_index[:, 1]), DH)
    result = attend_local(
        rotate(place(received[0]).reshape(shaped), cos_table, sin_table),
        rotate(place(received[1]).reshape(shaped), cos_table, sin_table),
        place(received[2]),
    )
    split = heads_here // 2
    head_count = lax.axis_size("head")
    me = lax.axis_index("head")
    partner_w = weight_block(out_weight, me ^ 1)
    own_w = weight_block(out_weight, me)

    def dot(lhs, weight):
        return jnp.dot(
            lhs, weight, precision=lax.Precision.HIGH, preferred_element_type=jnp.float32
        )

    def exchange(lo, hi):
        part = result[0 if lo == 0 else 1][picked]
        back = lax.all_to_all(part, "seq", split_axis=0, concat_axis=0, tiled=True)
        return back

    def half_terms(back, lo, hi, start_partner, start_own, hold):
        mixed = back[send_row].reshape(row_count, (hi - lo) * DH)
        far_mixed = lax.ppermute(mixed, "head", swap_pairs(head_count, 2))
        rows = slice(lo * DH, hi * DH)
        near_partner = dot(mixed, partner_w[rows])
        near_own = dot(mixed, own_w[rows])
        if start_partner is not None:
            near_partner = start_partner + near_partner
            near_own = start_own + near_own
        if hold:
            far_mixed, near_partner, near_own = lax.optimization_barrier(
                (far_mixed, near_partner, near_own)
            )
        to_partner = near_partner + dot(far_mixed, far_weights[1, rows])
        to_own = near_own + dot(far_mixed, far_weights[0, rows])
        return to_partner, to_own

    first_partner, first_own = half_terms(exchange(0, split), 0, split, None, None, False)
    second_back = exchange(split, heads_here)
    second_back, first_partner, first_own = lax.optimization_barrier(
        (second_back, first_partner, first_own)
    )
    for_partner, own = half_terms(
        second_back, split, heads_here, first_partner, first_own, True
    )
    from_partner = lax.ppermute(for_partner, "head", swap_pairs(head_count, 1))
    return own + from_partner


def swap_pairs(count, bit):
    return [(index, index ^ bit) for index in range(count)]


def weight_block(out_weight, index):
    width = out_weight.shape[1] // lax.axis_size("head")
    return lax.dynamic_slice_in_dim(out_weight, index * width, width, axis=1)


def fetch_far_weights(out_weight):
    head_count = lax.axis_size("head")
    me = lax.axis_index("head")
    outgoing = jnp.stack(
        [weight_block(out_weight, me ^ 2), weight_block(out_weight, me ^ 3)], 0
    )
    return lax.ppermute(outgoing, "head", swap_pairs(head_count, 2))


def solution(mesh):
    in_specs = (
        P("seq", "head"),
        P("seq", "head"),
        P("seq", "head"),
        P("seq"),
        P("seq"),
        P("seq"),
        P("head", None),
    )
    out_specs = P("seq", "head")
    return jax.shard_map(
        per_device, mesh=mesh, in_specs=in_specs, out_specs=out_specs, check_vma=False
    )
```

```python
import math

import jax
import jax.numpy as jnp
from jax import lax
from jax.sharding import PartitionSpec as P

DH = 128
CS = 1024
CL_DEV = 1


ROPE_BASE = 500000.0
ORIG_CONTEXT = 8192.0
STRETCH = 4.0
BETA_FAST = 32.0
BETA_SLOW = 1.0


def yarn_tables(token_pos, width):
    half_width = width // 2
    expo = jnp.arange(half_width, dtype=jnp.float32) * 2.0 / width
    theta = jnp.exp(-expo * math.log(ROPE_BASE))
    ratio = ORIG_CONTEXT * theta / (2.0 * math.pi)
    ramp = jnp.clip((ratio - BETA_SLOW) / (BETA_FAST - BETA_SLOW), 0.0, 1.0)
    freq = theta * (ramp + (1.0 - ramp) / STRETCH)
    angle = token_pos.astype(jnp.float32)[:, None] * freq[None, :]
    mscale = 0.1 * math.log(STRETCH) + 1.0
    cos_table = jnp.concatenate([jnp.cos(angle), jnp.cos(angle)], -1) * mscale
    sin_table = jnp.concatenate([jnp.sin(angle), jnp.sin(angle)], -1) * mscale
    return (cos_table[:, None, :], sin_table[:, None, :])


def rotate(field, cos_table, sin_table):
    half_width = field.shape[-1] // 2
    turned = jnp.concatenate([-field[..., half_width:], field[..., :half_width]], -1)
    return field * cos_table + turned * sin_table


def cluster_attention(triple):
    query_c, key_c, value_c = triple
    length = query_c.shape[0]
    scores = jnp.einsum(
        "qhd,khd->hqk", query_c, key_c, precision=lax.Precision.HIGH
    ) / math.sqrt(query_c.shape[-1])
    causal = jnp.arange(length)[:, None] >= jnp.arange(length)[None, :]
    scores = jnp.where(causal[None], scores, -jnp.inf)
    peak = jnp.max(scores, -1, keepdims=True)
    weights = jnp.exp(scores - peak)
    total = jnp.sum(weights, -1, keepdims=True)
    split = query_c.shape[1] // 2
    parts = []
    for (lo, hi), value_part in zip(((0, split), (split, query_c.shape[1])), value_c):
        summed = jnp.einsum(
            "hqk,khd->qhd", weights[lo:hi], value_part, precision=lax.Precision.HIGH
        )
        parts.append(summed / jnp.transpose(total[lo:hi], (1, 0, 2)))
    return tuple(parts)


def attend_local(query_all, key_all, value_all):
    row_count, head_count, width = query_all.shape
    grouped = (
        query_all.reshape(row_count // CS, CS, head_count, width),
        key_all.reshape(row_count // CS, CS, head_count, width),
        tuple(
            part.reshape(row_count // CS, CS, part.shape[1], width) for part in value_all
        ),
    )
    parts = lax.map(cluster_attention, grouped)
    return [part.reshape(row_count, part.shape[2], width) for part in parts]


def per_device(queries, keys, values, positions, cluster, slot, out_weight):
    seq_count = lax.axis_size("seq")
    row_count = queries.shape[0]
    capacity = 3 * row_count // (2 * seq_count)
    buffer_rows = seq_count * capacity
    heads_here = queries.shape[1] // DH
    owner_ids = cluster // CL_DEV
    target_row = cluster % CL_DEV * CS + slot
    one_hot = (owner_ids[:, None] == jnp.arange(seq_count)[None, :]).astype(jnp.int32)
    token_rank = jnp.sum(jnp.cumsum(one_hot, 0) * one_hot, 1) - 1
    send_row = owner_ids * capacity + token_rank
    source_token = (
        jnp.full((buffer_rows,), row_count, jnp.int32)
        .at[send_row]
        .set(jnp.arange(row_count, dtype=jnp.int32))
    )
    shaped = (row_count, heads_here, DH)
    send_from = jnp.minimum(source_token, row_count - 1)
    send_q = queries.reshape(shaped)[send_from]
    send_k = keys.reshape(shaped)[send_from]
    send_v = values.reshape(shaped)[send_from]
    index_rows = (
        jnp.full((buffer_rows, 2), row_count, jnp.int32)
        .at[send_row]
        .set(jnp.stack([target_row, positions], 1))
    )
    arrived_index = lax.all_to_all(index_rows, "seq", split_axis=0, concat_axis=0, tiled=True)
    arrived = arrived_index[:, 0]
    picked = jnp.minimum(arrived, row_count - 1)
    where_from = (
        jnp.zeros((row_count,), jnp.int32)
        .at[arrived]
        .set(jnp.arange(buffer_rows, dtype=jnp.int32), mode="drop")
    )

    def place(pieces):
        return pieces[where_from]

    far_weights = fetch_far_weights(out_weight)
    first_arrived = lax.all_to_all(send_q, "seq", split_axis=0, concat_axis=0, tiled=True)
    first_arrived, far_weights = lax.optimization_barrier((first_arrived, far_weights))
    received = (
        first_arrived,
        lax.all_to_all(send_k, "seq", split_axis=0, concat_axis=0, tiled=True),
        lax.all_to_all(send_v, "seq", split_axis=0, concat_axis=0, tiled=True),
    )
    split = heads_here // 2
    cos_table, sin_table = yarn_tables(place(arrived_index[:, 1]), DH)
    result = attend_local(
        rotate(place(received[0]), cos_table, sin_table),
        rotate(place(received[1]), cos_table, sin_table),
        tuple(place(received[2][:, lo:hi]) for lo, hi in ((0, split), (split, heads_here))),
    )
    split = heads_here // 2
    head_count = lax.axis_size("head")
    me = lax.axis_index("head")
    partner_w = weight_block(out_weight, me ^ 1)
    own_w = weight_block(out_weight, me)

    def dot(lhs, weight):
        return jnp.dot(
            lhs, weight, precision=lax.Precision.HIGH, preferred_element_type=jnp.float32
        )

    def exchange(lo, hi):
        part = result[0 if lo == 0 else 1][picked]
        back = lax.all_to_all(part, "seq", split_axis=0, concat_axis=0, tiled=True)
        return back

    def half_terms(back, lo, hi, start_partner, start_own, hold):
        mixed = back[send_row].reshape(row_count, (hi - lo) * DH)
        far_mixed = lax.ppermute(mixed, "head", swap_pairs(head_count, 2))
        rows = slice(lo * DH, hi * DH)
        near_partner = dot(mixed, partner_w[rows])
        near_own = dot(mixed, own_w[rows])
        if start_partner is not None:
            near_partner = start_partner + near_partner
            near_own = start_own + near_own
        if hold:
            far_mixed, near_partner, near_own = lax.optimization_barrier(
                (far_mixed, near_partner, near_own)
            )
        to_partner = near_partner + dot(far_mixed, far_weights[1, rows])
        to_own = near_own + dot(far_mixed, far_weights[0, rows])
        return to_partner, to_own

    first_partner, first_own = half_terms(exchange(0, split), 0, split, None, None, False)
    second_back = exchange(split, heads_here)
    second_back, first_partner, first_own = lax.optimization_barrier(
        (second_back, first_partner, first_own)
    )
    for_partner, own = half_terms(
        second_back, split, heads_here, first_partner, first_own, True
    )
    from_partner = lax.ppermute(for_partner, "head", swap_pairs(head_count, 1))
    return own + from_partner


def swap_pairs(count, bit):
    return [(index, index ^ bit) for index in range(count)]


def weight_block(out_weight, index):
    width = out_weight.shape[1] // lax.axis_size("head")
    return lax.dynamic_slice_in_dim(out_weight, index * width, width, axis=1)


def fetch_far_weights(out_weight):
    head_count = lax.axis_size("head")
    me = lax.axis_index("head")
    outgoing = jnp.stack(
        [weight_block(out_weight, me ^ 2), weight_block(out_weight, me ^ 3)], 0
    )
    return lax.ppermute(outgoing, "head", swap_pairs(head_count, 2))


def solution(mesh):
    in_specs = (
        P("seq", "head"),
        P("seq", "head"),
        P("seq", "head"),
        P("seq"),
        P("seq"),
        P("seq"),
        P("head", None),
    )
    out_specs = P("seq", "head")
    return jax.shard_map(
        per_device, mesh=mesh, in_specs=in_specs, out_specs=out_specs, check_vma=False
    )
```

```python
import math

import jax
import jax.numpy as jnp
from jax import lax
from jax.sharding import PartitionSpec as P

DH = 128
CS = 1024
CL_DEV = 1


ROPE_BASE = 500000.0
ORIG_CONTEXT = 8192.0
STRETCH = 4.0
BETA_FAST = 32.0
BETA_SLOW = 1.0


def yarn_tables(token_pos, width):
    half_width = width // 2
    expo = jnp.arange(half_width, dtype=jnp.float32) * 2.0 / width
    theta = jnp.exp(-expo * math.log(ROPE_BASE))
    ratio = ORIG_CONTEXT * theta / (2.0 * math.pi)
    ramp = jnp.clip((ratio - BETA_SLOW) / (BETA_FAST - BETA_SLOW), 0.0, 1.0)
    freq = theta * (ramp + (1.0 - ramp) / STRETCH)
    angle = token_pos.astype(jnp.float32)[:, None] * freq[None, :]
    mscale = 0.1 * math.log(STRETCH) + 1.0
    cos_table = jnp.concatenate([jnp.cos(angle), jnp.cos(angle)], -1) * mscale
    sin_table = jnp.concatenate([jnp.sin(angle), jnp.sin(angle)], -1) * mscale
    return (cos_table[:, None, :], sin_table[:, None, :])


def rotate(field, cos_table, sin_table):
    half_width = field.shape[-1] // 2
    turned = jnp.concatenate([-field[..., half_width:], field[..., :half_width]], -1)
    return field * cos_table + turned * sin_table


def cluster_attention(triple):
    query_c, key_c, value_c = triple
    length = query_c.shape[0]
    scores = jnp.einsum(
        "qhd,khd->hqk", query_c, key_c, precision=lax.Precision.HIGH
    ) / math.sqrt(query_c.shape[-1])
    causal = jnp.arange(length)[:, None] >= jnp.arange(length)[None, :]
    scores = jnp.where(causal[None], scores, -jnp.inf)
    peak = jnp.max(scores, -1, keepdims=True)
    weights = jnp.exp(scores - peak)
    total = jnp.sum(weights, -1, keepdims=True)
    split = query_c.shape[1] // 2
    parts = []
    for lo, hi in ((0, split), (split, query_c.shape[1])):
        summed = jnp.einsum(
            "hqk,khd->qhd", weights[lo:hi], value_c[:, lo:hi], precision=lax.Precision.HIGH
        )
        parts.append(summed / jnp.transpose(total[lo:hi], (1, 0, 2)))
    return tuple(parts)


def attend_local(query_all, key_all, value_all):
    row_count, head_count, width = query_all.shape
    grouped = (
        query_all.reshape(row_count // CS, CS, head_count, width),
        key_all.reshape(row_count // CS, CS, head_count, width),
        value_all.reshape(row_count // CS, CS, head_count, width),
    )
    parts = lax.map(cluster_attention, grouped)
    return [part.reshape(row_count, part.shape[2], width) for part in parts]


def per_device(queries, keys, values, positions, cluster, slot, out_weight):
    seq_count = lax.axis_size("seq")
    row_count = queries.shape[0]
    capacity = 3 * row_count // (2 * seq_count)
    buffer_rows = seq_count * capacity
    heads_here = queries.shape[1] // DH
    owner_ids = cluster // CL_DEV
    target_row = cluster % CL_DEV * CS + slot
    one_hot = (owner_ids[:, None] == jnp.arange(seq_count)[None, :]).astype(jnp.int32)
    token_rank = jnp.sum(jnp.cumsum(one_hot, 0) * one_hot, 1) - 1
    send_row = owner_ids * capacity + token_rank
    source_token = (
        jnp.full((buffer_rows,), row_count, jnp.int32)
        .at[send_row]
        .set(jnp.arange(row_count, dtype=jnp.int32))
    )
    shaped = (row_count, heads_here, DH)
    send_from = jnp.minimum(source_token, row_count - 1)
    send_q = queries.reshape(shaped)[send_from]
    send_k = keys.reshape(shaped)[send_from]
    send_v = values.reshape(shaped)[send_from]
    index_rows = (
        jnp.full((buffer_rows, 2), row_count, jnp.int32)
        .at[send_row]
        .set(jnp.stack([target_row, positions], 1))
    )
    arrived_index = lax.all_to_all(index_rows, "seq", split_axis=0, concat_axis=0, tiled=True)
    arrived = arrived_index[:, 0]
    picked = jnp.minimum(arrived, row_count - 1)
    where_from = (
        jnp.zeros((row_count,), jnp.int32)
        .at[arrived]
        .set(jnp.arange(buffer_rows, dtype=jnp.int32), mode="drop")
    )

    def place(pieces):
        return pieces[where_from]

    far_weights = fetch_far_weights(out_weight)
    first_arrived = lax.all_to_all(send_q, "seq", split_axis=0, concat_axis=0, tiled=True)
    first_arrived, far_weights = lax.optimization_barrier((first_arrived, far_weights))
    received = (
        first_arrived,
        lax.all_to_all(send_k, "seq", split_axis=0, concat_axis=0, tiled=True),
        lax.all_to_all(send_v, "seq", split_axis=0, concat_axis=0, tiled=True),
    )
    cos_table, sin_table = yarn_tables(place(arrived_index[:, 1]), DH)
    result = attend_local(
        rotate(place(received[0]), cos_table, sin_table),
        rotate(place(received[1]), cos_table, sin_table),
        place(received[2]),
    )
    split = heads_here // 2
    head_count = lax.axis_size("head")
    me = lax.axis_index("head")
    partner_w = weight_block(out_weight, me ^ 1)
    own_w = weight_block(out_weight, me)

    def dot(lhs, weight):
        return jnp.dot(
            lhs, weight, precision=lax.Precision.HIGH, preferred_element_type=jnp.float32
        )

    def exchange(lo, hi):
        part = result[0 if lo == 0 else 1][picked]
        back = lax.all_to_all(part, "seq", split_axis=0, concat_axis=0, tiled=True)
        return back

    def half_terms(back, lo, hi, start_partner, start_own, hold):
        mixed = back[send_row].reshape(row_count, (hi - lo) * DH)
        far_mixed = lax.ppermute(mixed, "head", swap_pairs(head_count, 2))
        rows = slice(lo * DH, hi * DH)
        near_partner = dot(mixed, partner_w[rows])
        near_own = dot(mixed, own_w[rows])
        if start_partner is not None:
            near_partner = start_partner + near_partner
            near_own = start_own + near_own
        if hold:
            far_mixed, near_partner, near_own = lax.optimization_barrier(
                (far_mixed, near_partner, near_own)
            )
        to_partner = near_partner + dot(far_mixed, far_weights[1, rows])
        return to_partner, near_own, far_mixed, rows

    first_partner, first_near, first_far, first_rows = half_terms(
        exchange(0, split), 0, split, None, None, False
    )
    first_own = first_near + dot(first_far, far_weights[0, first_rows])
    second_back = exchange(split, heads_here)
    second_back, first_partner, first_own = lax.optimization_barrier(
        (second_back, first_partner, first_own)
    )
    for_partner, near_own, far_mixed, rows = half_terms(
        second_back, split, heads_here, first_partner, first_own, True
    )
    from_partner = lax.ppermute(for_partner, "head", swap_pairs(head_count, 1))
    return (near_own + from_partner) + dot(far_mixed, far_weights[0, rows])


def swap_pairs(count, bit):
    return [(index, index ^ bit) for index in range(count)]


def weight_block(out_weight, index):
    width = out_weight.shape[1] // lax.axis_size("head")
    return lax.dynamic_slice_in_dim(out_weight, index * width, width, axis=1)


def fetch_far_weights(out_weight):
    head_count = lax.axis_size("head")
    me = lax.axis_index("head")
    outgoing = jnp.stack(
        [weight_block(out_weight, me ^ 2), weight_block(out_weight, me ^ 3)], 0
    )
    return lax.ppermute(outgoing, "head", swap_pairs(head_count, 2))


def solution(mesh):
    in_specs = (
        P("seq", "head"),
        P("seq", "head"),
        P("seq", "head"),
        P("seq"),
        P("seq"),
        P("seq"),
        P("head", None),
    )
    out_specs = P("seq", "head")
    return jax.shard_map(
        per_device, mesh=mesh, in_specs=in_specs, out_specs=out_specs, check_vma=False
    )
```
